256 devices in a mesh: vel: 16 (over y, z_lo), space: 16 (over x, z_hi, core).
Axes of the slice: x: 4, y: 4, z: 8 (z_hi: 2, z_lo: 4; z = z_hi * 4 + z_lo), core: 2. Of those that a mesh axis runs over, the one named last changes fastest.
Arguments:
- initial: float32 [13824, 64, 128], P('vel', 'space'), as said below
- site_kind: int32 [64, 128], P('space'), may hold values from 0 to 2, as said below
Outputs:
- distribution: float32 [13824, 64, 128], P('vel', 'space')
- kelvin_level: float32 [64, 128], P('space')
The draws below stay inside these ranges and needn't reach their ends.
Inputs may be any that keep to these rules, and one draw needn't show every extreme that they name: `site_kind`: 0 marks a gas cell, 1 a wall cell, 2 an inflow cell. `initial`: every entry is positive.
All inputs are finite; a program needn't handle non-finite values.
Results may differ from the reference program's by a relative error of at most 0.0003.
Values sent between devices are 32-bit elements; how exact they have to be, the bound alone decides.
No kernel may reach another device: no remote copies, remote signals or barrier semaphores. Data moves between devices by JAX's collectives and lax.ppermute only.
A program may use at most 64 MiB of HBM per device.

```python
import math
import jax
import jax.numpy as jnp
from jax import lax

NVX = 24
NODES_LATTICE = 13824
GRID_ROWS_Y = 128
STEPS = 2
GRID_ROWS_X = 64


def draw_initial(key, part):
    stochastic_seed_list = jax.random.split(key, 6)
    index = jnp.arange(NODES_LATTICE, dtype=jnp.int32)
    spacing = 8.0 / (NVX - 1)
    along_x_part = (-4.0 + spacing * (index // (NVX * NVX)).astype(jnp.float32))[:, None, None]
    along_y_part = (-4.0 + spacing * (index // NVX % NVX).astype(jnp.float32))[:, None, None]
    along_z_part = (-4.0 + spacing * (index % NVX).astype(jnp.float32))[:, None, None]
    particle_concentration = jnp.exp(jax.random.uniform(stochastic_seed_list[0], (GRID_ROWS_X, GRID_ROWS_Y), minval=math.log(0.4), maxval=math.log(2.5)))
    drift_range = 0.6
    jitter_low = 0.6
    jitter_high = 1.4
    average_drift_x = jax.random.uniform(stochastic_seed_list[1], (GRID_ROWS_X, GRID_ROWS_Y), minval=-drift_range, maxval=drift_range)
    average_drift_y = jax.random.uniform(stochastic_seed_list[2], (GRID_ROWS_X, GRID_ROWS_Y), minval=-drift_range, maxval=drift_range)
    average_drift_z = jax.random.uniform(stochastic_seed_list[3], (GRID_ROWS_X, GRID_ROWS_Y), minval=-drift_range, maxval=drift_range)
    kelvin_level = jnp.exp(jax.random.uniform(stochastic_seed_list[4], (GRID_ROWS_X, GRID_ROWS_Y), minval=math.log(0.6), maxval=math.log(1.8)))
    kinetic_variance = (along_x_part - average_drift_x[None]) ** 2 + (along_y_part - average_drift_y[None]) ** 2 + (along_z_part - average_drift_z[None]) ** 2
    gaussian_local_balance = particle_concentration[None] * kelvin_level[None] ** (-1.5) * jnp.exp(-kinetic_variance / (2.0 * kelvin_level[None]))
    jitter = jax.random.uniform(stochastic_seed_list[5], (NODES_LATTICE, GRID_ROWS_X, GRID_ROWS_Y), minval=jitter_low, maxval=jitter_high)
    return (gaussian_local_balance * jitter).astype(jnp.float32)


def draw_site_kind(key, part):
    levels = jax.random.randint(key, (GRID_ROWS_X, GRID_ROWS_Y), 0, 10)
    kind_labels = jnp.where(levels < 8, 0, jnp.where(levels < 9, 1, 2)).astype(jnp.int32)
    return kind_labels.at[0, 0].set(1).at[0, 1].set(2)


def setup_inputs(seed: int = 0) -> dict:
    key_list = jax.random.split(jax.random.key(seed), 3)
    initial = draw_initial(jax.random.fold_in(key_list[2], 71), 0)
    site_kind = draw_site_kind(jax.random.fold_in(key_list[2], 71), 0)
    return dict(initial=initial, site_kind=site_kind)


speed_limit = 4.0
courant = 0.1
diffusivity_ratio = 2.0 / 3.0
power_law_index = 0.81
encounter_rate = 0.25
wall_kelvin = 1.0
inflow_concentration = 1.0
inflow_speed = 0.5
inflow_kelvin = 1.0


def speeds(offset, amount):
    index = offset + jnp.arange(amount, dtype=jnp.int32)
    spacing = 2.0 * speed_limit / (NVX - 1)
    along_x_part = -speed_limit + spacing * (index // (NVX * NVX)).astype(jnp.float32)
    along_y_part = -speed_limit + spacing * ((index // NVX) % NVX).astype(jnp.float32)
    along_z_part = -speed_limit + spacing * (index % NVX).astype(jnp.float32)
    return along_x_part, along_y_part, along_z_part


def quad_weight():
    return (2.0 * speed_limit / (NVX - 1)) ** 3 / (2.0 * math.pi) ** 1.5


def minmod(left, right):
    return 0.5 * (jnp.sign(left) + jnp.sign(right)) * jnp.minimum(jnp.abs(left), jnp.abs(right))


def sweep(distribution_table, number, along):
    length = distribution_table.shape[along]

    def piece(source, low, high):
        return lax.slice_in_dim(source, low, high, axis=along)

    jumps = piece(distribution_table, 1, length) - piece(distribution_table, 0, length - 1)
    slopes = minmod(piece(jumps, 0, length - 2), piece(jumps, 1, length - 1))
    left_face = piece(distribution_table, 1, length - 2) + 0.5 * (1.0 - number) * piece(slopes, 0, length - 3)
    right_face = piece(distribution_table, 2, length - 1) - 0.5 * (1.0 + number) * piece(slopes, 1, length - 2)
    flux = number * jnp.where(number > 0, left_face, right_face)
    return piece(distribution_table, 2, length - 2) - (piece(flux, 1, length - 3) - piece(flux, 0, length - 4))


def transport(padded, along_x_part, along_y_part):
    swept = sweep(padded, courant * along_x_part[:, None, None], 1)
    widened = jnp.pad(swept, ((0, 0), (0, 0), (2, 2)))
    return sweep(widened, courant * along_y_part[:, None, None], 2)


def raw_table(along_x_part, along_y_part, along_z_part):
    magnitude_squares = along_x_part * along_x_part + along_y_part * along_y_part + along_z_part * along_z_part
    return quad_weight() * jnp.stack([jnp.ones_like(along_x_part), along_x_part, along_y_part, along_z_part, magnitude_squares])


def flow_drift_vector(integral_totals):
    particle_concentration = integral_totals[0]
    average_drift_x = integral_totals[1] / particle_concentration
    average_drift_y = integral_totals[2] / particle_concentration
    average_drift_z = integral_totals[3] / particle_concentration
    kelvin_level = (integral_totals[4] / particle_concentration - (average_drift_x * average_drift_x + average_drift_y * average_drift_y + average_drift_z * average_drift_z)) / 3.0
    return particle_concentration, average_drift_x, average_drift_y, average_drift_z, kelvin_level


def heat_terms(advected_distribution, along_x_part, along_y_part, along_z_part, average_drift_x, average_drift_y, average_drift_z):
    rel_x = along_x_part[:, None, None] - average_drift_x[None]
    rel_y = along_y_part[:, None, None] - average_drift_y[None]
    rel_z = along_z_part[:, None, None] - average_drift_z[None]
    scaled = 0.5 * quad_weight() * (rel_x * rel_x + rel_y * rel_y + rel_z * rel_z) * advected_distribution
    return jnp.stack([jnp.sum(rel_x * scaled, axis=0), jnp.sum(rel_y * scaled, axis=0), jnp.sum(rel_z * scaled, axis=0)])


def perform_relaxing(advected_distribution, kind_labels, along_x_part, along_y_part, along_z_part, particle_concentration, average_drift_x, average_drift_y, average_drift_z, kelvin_level, conductive_transfer):
    rel_x = along_x_part[:, None, None] - average_drift_x[None]
    rel_y = along_y_part[:, None, None] - average_drift_y[None]
    rel_z = along_z_part[:, None, None] - average_drift_z[None]
    relative_magnitude_square = rel_x * rel_x + rel_y * rel_y + rel_z * rel_z
    stress_scalar_grid = particle_concentration * kelvin_level
    gaussian_local_balance = particle_concentration * kelvin_level ** -1.5 * jnp.exp(-relative_magnitude_square / (2.0 * kelvin_level))
    conductive_vector_slot = rel_x * conductive_transfer[0] + rel_y * conductive_transfer[1] + rel_z * conductive_transfer[2]
    corrected_goal_distribution = gaussian_local_balance * (1.0 + (1.0 - diffusivity_ratio) * conductive_vector_slot * (relative_magnitude_square / kelvin_level - 5.0) / (5.0 * stress_scalar_grid * kelvin_level))
    approach_rate = encounter_rate * particle_concentration * kelvin_level ** (1.0 - power_law_index)
    relaxed = advected_distribution + approach_rate * (corrected_goal_distribution - advected_distribution)
    magnitude_squares = (along_x_part * along_x_part + along_y_part * along_y_part + along_z_part * along_z_part)[:, None, None]
    wall_distribution = particle_concentration * wall_kelvin ** -1.5 * jnp.exp(-magnitude_squares / (2.0 * wall_kelvin))
    inflow_magnitude_square = ((along_x_part - inflow_speed) ** 2 + along_y_part * along_y_part + along_z_part * along_z_part)[:, None, None]
    inflow_distribution = inflow_concentration * inflow_kelvin ** -1.5 * jnp.exp(-inflow_magnitude_square / (2.0 * inflow_kelvin))
    return jnp.where(kind_labels == 1, wall_distribution, jnp.where(kind_labels == 2, inflow_distribution, relaxed))


def reference(initial, site_kind):
    block = NVX * NVX
    distribution_table = initial.reshape(NVX, block, GRID_ROWS_X, GRID_ROWS_Y)
    starts = jnp.arange(NVX, dtype=jnp.int32) * block
    kelvin_level = jnp.zeros((GRID_ROWS_X, GRID_ROWS_Y), jnp.float32)
    for section in range(STEPS):
        def move_block(inputs):
            tile_elements, offset = inputs
            along_x_part, along_y_part, along_z_part = speeds(offset, block)
            padded = jnp.pad(tile_elements, ((0, 0), (2, 2), (0, 0)))
            advected_distribution = transport(padded, along_x_part, along_y_part)
            cumulative_total = jnp.einsum("kv,vrc->krc", raw_table(along_x_part, along_y_part, along_z_part), advected_distribution, precision=lax.Precision.HIGHEST)
            return advected_distribution, cumulative_total

        advected_distribution, cumulative_total = lax.map(move_block, (distribution_table, starts))
        particle_concentration, average_drift_x, average_drift_y, average_drift_z, kelvin_level = flow_drift_vector(jnp.sum(cumulative_total, axis=0))

        def heat_block(inputs):
            tile_elements, offset = inputs
            along_x_part, along_y_part, along_z_part = speeds(offset, block)
            return heat_terms(tile_elements, along_x_part, along_y_part, along_z_part, average_drift_x, average_drift_y, average_drift_z)

        conductive_transfer = jnp.sum(lax.map(heat_block, (advected_distribution, starts)), axis=0)

        def collide_block(inputs):
            tile_elements, offset = inputs
            along_x_part, along_y_part, along_z_part = speeds(offset, block)
            return perform_relaxing(tile_elements, site_kind, along_x_part, along_y_part, along_z_part, particle_concentration, average_drift_x, average_drift_y, average_drift_z, kelvin_level, conductive_transfer)

        distribution_table = lax.map(collide_block, (advected_distribution, starts))
    return distribution_table.reshape(NODES_LATTICE, GRID_ROWS_X, GRID_ROWS_Y), kelvin_level
```

```python
import math

import jax
import jax.numpy as jnp
from jax import lax
from jax.sharding import PartitionSpec as P

NVX = 24
STEPS = 2


speed_limit = 4.0
courant = 0.1
diffusivity_ratio = 2.0 / 3.0
power_law_index = 0.81
encounter_rate = 0.25
wall_kelvin = 1.0
inflow_concentration = 1.0
inflow_speed = 0.5
inflow_kelvin = 1.0


def with_halo(block, sides, width):
    for axis, dim in sides:
        count = lax.axis_size(axis)
        forward = [(i, i + 1) for i in range(count - 1)]
        backward = [(target, source) for source, target in forward]
        low = lax.ppermute(
            lax.slice_in_dim(block, block.shape[dim] - width, None, axis=dim), axis, forward
        )
        high = lax.ppermute(lax.slice_in_dim(block, 0, width, axis=dim), axis, backward)
        block = jnp.concatenate([low, block, high], axis=dim)
    return block


def speeds(offset, amount):
    index = offset + jnp.arange(amount, dtype=jnp.int32)
    spacing = 2.0 * speed_limit / (NVX - 1)
    along_x_part = -speed_limit + spacing * (index // (NVX * NVX)).astype(jnp.float32)
    along_y_part = -speed_limit + spacing * (index // NVX % NVX).astype(jnp.float32)
    along_z_part = -speed_limit + spacing * (index % NVX).astype(jnp.float32)
    return (along_x_part, along_y_part, along_z_part)


def quad_weight():
    return (2.0 * speed_limit / (NVX - 1)) ** 3 / (2.0 * math.pi) ** 1.5


def minmod(left, right):
    return 0.5 * (jnp.sign(left) + jnp.sign(right)) * jnp.minimum(jnp.abs(left), jnp.abs(right))


def sweep(distribution_table, number, along):
    length = distribution_table.shape[along]

    def piece(source, low, high):
        return lax.slice_in_dim(source, low, high, axis=along)

    jumps = piece(distribution_table, 1, length) - piece(distribution_table, 0, length - 1)
    slopes = minmod(piece(jumps, 0, length - 2), piece(jumps, 1, length - 1))
    left_face = piece(distribution_table, 1, length - 2) + 0.5 * (1.0 - number) * piece(
        slopes, 0, length - 3
    )
    right_face = piece(distribution_table, 2, length - 1) - 0.5 * (1.0 + number) * piece(
        slopes, 1, length - 2
    )
    flux = number * jnp.where(number > 0, left_face, right_face)
    return piece(distribution_table, 2, length - 2) - (
        piece(flux, 1, length - 3) - piece(flux, 0, length - 4)
    )


def transport(padded, along_x_part, along_y_part):
    swept = sweep(padded, courant * along_x_part[:, None, None], 1)
    widened = jnp.pad(swept, ((0, 0), (0, 0), (2, 2)))
    return sweep(widened, courant * along_y_part[:, None, None], 2)


def xor_tree(values):
    while len(values) > 1:
        values = [values[2 * j] + values[2 * j + 1] for j in range(len(values) // 2)]
    return values[0]


def vel_sum(local):
    count = lax.axis_size("vel")
    if count & (count - 1):
        return lax.psum(local, "vel")
    bits = count.bit_length() - 1
    low = 0
    while low < bits:
        width = min(2, bits - low)
        values = [local]
        for member in range(1, 1 << width):
            mask = member << low
            values.append(lax.ppermute(local, "vel", [(i, i ^ mask) for i in range(count)]))
        local = xor_tree(values)
        low += width
    return local


def macroscopic_moments(advected_distribution, along_x_part, along_y_part, along_z_part):
    magnitude_squares = (
        along_x_part * along_x_part + along_y_part * along_y_part + along_z_part * along_z_part
    )
    ones = jnp.ones_like(along_x_part)
    table = quad_weight() * jnp.stack(
        [
            ones,
            along_x_part,
            along_y_part,
            along_z_part,
            magnitude_squares,
            along_x_part * along_x_part,
            along_y_part * along_y_part,
            along_z_part * along_z_part,
            along_x_part * along_y_part,
            along_x_part * along_z_part,
            along_y_part * along_z_part,
            along_x_part * magnitude_squares,
            along_y_part * magnitude_squares,
            along_z_part * magnitude_squares,
            jnp.zeros_like(along_x_part),
            jnp.zeros_like(along_x_part),
        ]
    )
    local = jnp.einsum("kv,vrc->krc", table, advected_distribution, precision=lax.Precision.HIGHEST)
    totals = vel_sum(local)
    particle_concentration = totals[0]
    average_drift_x = totals[1] / particle_concentration
    average_drift_y = totals[2] / particle_concentration
    average_drift_z = totals[3] / particle_concentration
    energy = totals[4]
    drift_square = (
        average_drift_x * average_drift_x
        + average_drift_y * average_drift_y
        + average_drift_z * average_drift_z
    )
    kelvin_level = (energy / particle_concentration - drift_square) / 3.0
    xx, yy, zz, xy, xz, yz = (totals[k] for k in range(5, 11))
    drift = (average_drift_x, average_drift_y, average_drift_z)
    second = ((xx, xy, xz), (xy, yy, yz), (xz, yz, zz))
    common = 2.0 * particle_concentration * drift_square
    conductive_transfer = jnp.stack(
        [
            0.5
            * (
                totals[11 + i]
                - 2.0 * (drift[0] * second[i][0] + drift[1] * second[i][1] + drift[2] * second[i][2])
                - drift[i] * energy
                + drift[i] * common
            )
            for i in range(3)
        ]
    )
    return (
        particle_concentration,
        average_drift_x,
        average_drift_y,
        average_drift_z,
        kelvin_level,
        conductive_transfer,
    )


def approach_increment(
    advected_distribution, kind_labels, along_x_part, along_y_part, along_z_part
):
    (
        particle_concentration,
        average_drift_x,
        average_drift_y,
        average_drift_z,
        kelvin_level,
        conductive_transfer,
    ) = macroscopic_moments(advected_distribution, along_x_part, along_y_part, along_z_part)
    rel_x = along_x_part[:, None, None] - average_drift_x[None]
    rel_y = along_y_part[:, None, None] - average_drift_y[None]
    rel_z = along_z_part[:, None, None] - average_drift_z[None]
    relative_magnitude_square = rel_x * rel_x + rel_y * rel_y + rel_z * rel_z
    stress_scalar_grid = particle_concentration * kelvin_level
    gaussian_local_balance = (
        particle_concentration
        * kelvin_level ** (-1.5)
        * jnp.exp(-relative_magnitude_square / (2.0 * kelvin_level))
    )
    conductive_vector_slot = (
        rel_x * conductive_transfer[0]
        + rel_y * conductive_transfer[1]
        + rel_z * conductive_transfer[2]
    )
    corrected_goal_distribution = gaussian_local_balance * (
        1.0
        + (1.0 - diffusivity_ratio)
        * conductive_vector_slot
        * (relative_magnitude_square / kelvin_level - 5.0)
        / (5.0 * stress_scalar_grid * kelvin_level)
    )
    approach_rate = (
        encounter_rate * particle_concentration * kelvin_level ** (1.0 - power_law_index)
    )
    relaxed = advected_distribution + approach_rate * (
        corrected_goal_distribution - advected_distribution
    )
    magnitude_squares = (
        along_x_part * along_x_part + along_y_part * along_y_part + along_z_part * along_z_part
    )[:, None, None]
    wall_distribution = (
        particle_concentration
        * wall_kelvin ** (-1.5)
        * jnp.exp(-magnitude_squares / (2.0 * wall_kelvin))
    )
    inflow_magnitude_square = (
        (along_x_part - inflow_speed) ** 2
        + along_y_part * along_y_part
        + along_z_part * along_z_part
    )[:, None, None]
    inflow_distribution = (
        inflow_concentration
        * inflow_kelvin ** (-1.5)
        * jnp.exp(-inflow_magnitude_square / (2.0 * inflow_kelvin))
    )
    revised_distribution = jnp.where(
        kind_labels == 1,
        wall_distribution,
        jnp.where(kind_labels == 2, inflow_distribution, relaxed),
    )
    return (revised_distribution, kelvin_level)


def per_device(initial, site_kind):
    amount = initial.shape[0]
    along_x_part, along_y_part, along_z_part = speeds(lax.axis_index("vel") * amount, amount)
    distribution_table = initial
    kelvin_level = jnp.zeros(site_kind.shape, jnp.float32)
    for section in range(STEPS):
        padded = with_halo(distribution_table, (("space", 1),), 2)
        advected_distribution = transport(padded, along_x_part, along_y_part)
        distribution_table, kelvin_level = approach_increment(
            advected_distribution, site_kind, along_x_part, along_y_part, along_z_part
        )
    return (distribution_table, kelvin_level)


def solution(mesh):
    return jax.shard_map(
        per_device,
        mesh=mesh,
        in_specs=(P("vel", "space", None), P("space", None)),
        out_specs=(P("vel", "space", None), P("space", None)),
        check_vma=False,
    )
```

```python
import math

import jax
import numpy as np
import jax.numpy as jnp
from jax import lax
from jax.sharding import PartitionSpec as P

NVX = 24
STEPS = 2


speed_limit = 4.0
courant = 0.1
diffusivity_ratio = 2.0 / 3.0
power_law_index = 0.81
encounter_rate = 0.25
wall_kelvin = 1.0
inflow_concentration = 1.0
inflow_speed = 0.5
inflow_kelvin = 1.0


def with_halo(block, sides, width):
    for axis, dim in sides:
        count = lax.axis_size(axis)
        forward = [(i, i + 1) for i in range(count - 1)]
        backward = [(target, source) for source, target in forward]
        low = lax.ppermute(
            lax.slice_in_dim(block, block.shape[dim] - width, None, axis=dim), axis, forward
        )
        high = lax.ppermute(lax.slice_in_dim(block, 0, width, axis=dim), axis, backward)
        block = jnp.concatenate([low, block, high], axis=dim)
    return block


def halo_signs(vel_count, amount):
    spacing = 2.0 * speed_limit / (NVX - 1)
    signs = []
    for member in range(vel_count):
        index = np.arange(member * amount, (member + 1) * amount)
        along_x_part = np.float32(-speed_limit) + np.float32(spacing) * (index // (NVX * NVX)).astype(np.float32)
        if np.all(along_x_part > 0):
            signs.append(1)
        elif np.all(along_x_part < 0):
            signs.append(-1)
        else:
            return None
    return signs


def with_upwind_halo(block, signs):
    count = lax.axis_size("space")
    rows = block.shape[1]
    forward = [(i, i + 1) for i in range(count - 1)]
    backward = [(target, source) for source, target in forward]
    low = lax.ppermute(block[:, rows - 1 :], "space", forward)
    high = lax.ppermute(block[:, :1], "space", backward)
    pairs = []
    for member, sign in enumerate(signs):
        for source, target in forward if sign > 0 else backward:
            pairs.append((member * count + source, member * count + target))
    positive = jnp.asarray(np.array(signs, np.int32))[lax.axis_index("vel")] > 0
    extra = lax.ppermute(
        jnp.where(positive, block[:, rows - 2 : rows - 1], block[:, 1:2]), ("vel", "space"), pairs
    )
    return jnp.concatenate([extra, low, block, high, extra], axis=1)


def speeds(offset, amount):
    index = offset + jnp.arange(amount, dtype=jnp.int32)
    spacing = 2.0 * speed_limit / (NVX - 1)
    along_x_part = -speed_limit + spacing * (index // (NVX * NVX)).astype(jnp.float32)
    along_y_part = -speed_limit + spacing * (index // NVX % NVX).astype(jnp.float32)
    along_z_part = -speed_limit + spacing * (index % NVX).astype(jnp.float32)
    return (along_x_part, along_y_part, along_z_part)


def quad_weight():
    return (2.0 * speed_limit / (NVX - 1)) ** 3 / (2.0 * math.pi) ** 1.5


def minmod(left, right):
    return 0.5 * (jnp.sign(left) + jnp.sign(right)) * jnp.minimum(jnp.abs(left), jnp.abs(right))


def sweep(distribution_table, number, along):
    length = distribution_table.shape[along]

    def piece(source, low, high):
        return lax.slice_in_dim(source, low, high, axis=along)

    jumps = piece(distribution_table, 1, length) - piece(distribution_table, 0, length - 1)
    slopes = minmod(piece(jumps, 0, length - 2), piece(jumps, 1, length - 1))
    left_face = piece(distribution_table, 1, length - 2) + 0.5 * (1.0 - number) * piece(
        slopes, 0, length - 3
    )
    right_face = piece(distribution_table, 2, length - 1) - 0.5 * (1.0 + number) * piece(
        slopes, 1, length - 2
    )
    flux = number * jnp.where(number > 0, left_face, right_face)
    return piece(distribution_table, 2, length - 2) - (
        piece(flux, 1, length - 3) - piece(flux, 0, length - 4)
    )


def transport(padded, along_x_part, along_y_part):
    swept = sweep(padded, courant * along_x_part[:, None, None], 1)
    widened = jnp.pad(swept, ((0, 0), (0, 0), (2, 2)))
    return sweep(widened, courant * along_y_part[:, None, None], 2)


def xor_tree(values):
    while len(values) > 1:
        values = [values[2 * j] + values[2 * j + 1] for j in range(len(values) // 2)]
    return values[0]


def vel_sum(local):
    count = lax.axis_size("vel")
    if count & (count - 1):
        return lax.psum(local, "vel")
    bits = count.bit_length() - 1
    low = 0
    while low < bits:
        width = min(2, bits - low)
        values = [local]
        for member in range(1, 1 << width):
            mask = member << low
            values.append(lax.ppermute(local, "vel", [(i, i ^ mask) for i in range(count)]))
        local = xor_tree(values)
        low += width
    return local


def macroscopic_moments(advected_distribution, along_x_part, along_y_part, along_z_part):
    magnitude_squares = (
        along_x_part * along_x_part + along_y_part * along_y_part + along_z_part * along_z_part
    )
    ones = jnp.ones_like(along_x_part)
    table = quad_weight() * jnp.stack(
        [
            ones,
            along_x_part,
            along_y_part,
            along_z_part,
            magnitude_squares,
            along_x_part * along_x_part,
            along_y_part * along_y_part,
            along_z_part * along_z_part,
            along_x_part * along_y_part,
            along_x_part * along_z_part,
            along_y_part * along_z_part,
            along_x_part * magnitude_squares,
            along_y_part * magnitude_squares,
            along_z_part * magnitude_squares,
            jnp.zeros_like(along_x_part),
            jnp.zeros_like(along_x_part),
        ]
    )
    local = jnp.einsum("kv,vrc->krc", table, advected_distribution, precision=lax.Precision.HIGHEST)
    totals = vel_sum(local)
    particle_concentration = totals[0]
    average_drift_x = totals[1] / particle_concentration
    average_drift_y = totals[2] / particle_concentration
    average_drift_z = totals[3] / particle_concentration
    energy = totals[4]
    drift_square = (
        average_drift_x * average_drift_x
        + average_drift_y * average_drift_y
        + average_drift_z * average_drift_z
    )
    kelvin_level = (energy / particle_concentration - drift_square) / 3.0
    xx, yy, zz, xy, xz, yz = (totals[k] for k in range(5, 11))
    drift = (average_drift_x, average_drift_y, average_drift_z)
    second = ((xx, xy, xz), (xy, yy, yz), (xz, yz, zz))
    common = 2.0 * particle_concentration * drift_square
    conductive_transfer = jnp.stack(
        [
            0.5
            * (
                totals[11 + i]
                - 2.0 * (drift[0] * second[i][0] + drift[1] * second[i][1] + drift[2] * second[i][2])
                - drift[i] * energy
                + drift[i] * common
            )
            for i in range(3)
        ]
    )
    return (
        particle_concentration,
        average_drift_x,
        average_drift_y,
        average_drift_z,
        kelvin_level,
        conductive_transfer,
    )


def approach_increment(
    advected_distribution, kind_labels, along_x_part, along_y_part, along_z_part
):
    (
        particle_concentration,
        average_drift_x,
        average_drift_y,
        average_drift_z,
        kelvin_level,
        conductive_transfer,
    ) = macroscopic_moments(advected_distribution, along_x_part, along_y_part, along_z_part)
    rel_x = along_x_part[:, None, None] - average_drift_x[None]
    rel_y = along_y_part[:, None, None] - average_drift_y[None]
    rel_z = along_z_part[:, None, None] - average_drift_z[None]
    relative_magnitude_square = rel_x * rel_x + rel_y * rel_y + rel_z * rel_z
    stress_scalar_grid = particle_concentration * kelvin_level
    gaussian_local_balance = (
        particle_concentration
        * kelvin_level ** (-1.5)
        * jnp.exp(-relative_magnitude_square / (2.0 * kelvin_level))
    )
    conductive_vector_slot = (
        rel_x * conductive_transfer[0]
        + rel_y * conductive_transfer[1]
        + rel_z * conductive_transfer[2]
    )
    corrected_goal_distribution = gaussian_local_balance * (
        1.0
        + (1.0 - diffusivity_ratio)
        * conductive_vector_slot
        * (relative_magnitude_square / kelvin_level - 5.0)
        / (5.0 * stress_scalar_grid * kelvin_level)
    )
    approach_rate = (
        encounter_rate * particle_concentration * kelvin_level ** (1.0 - power_law_index)
    )
    relaxed = advected_distribution + approach_rate * (
        corrected_goal_distribution - advected_distribution
    )
    magnitude_squares = (
        along_x_part * along_x_part + along_y_part * along_y_part + along_z_part * along_z_part
    )[:, None, None]
    wall_distribution = (
        particle_concentration
        * wall_kelvin ** (-1.5)
        * jnp.exp(-magnitude_squares / (2.0 * wall_kelvin))
    )
    inflow_magnitude_square = (
        (along_x_part - inflow_speed) ** 2
        + along_y_part * along_y_part
        + along_z_part * along_z_part
    )[:, None, None]
    inflow_distribution = (
        inflow_concentration
        * inflow_kelvin ** (-1.5)
        * jnp.exp(-inflow_magnitude_square / (2.0 * inflow_kelvin))
    )
    revised_distribution = jnp.where(
        kind_labels == 1,
        wall_distribution,
        jnp.where(kind_labels == 2, inflow_distribution, relaxed),
    )
    return (revised_distribution, kelvin_level)


def per_device(initial, site_kind):
    amount = initial.shape[0]
    along_x_part, along_y_part, along_z_part = speeds(lax.axis_index("vel") * amount, amount)
    distribution_table = initial
    kelvin_level = jnp.zeros(site_kind.shape, jnp.float32)
    signs = halo_signs(lax.axis_size("vel"), amount)
    for section in range(STEPS):
        if signs is None or distribution_table.shape[1] < 2:
            padded = with_halo(distribution_table, (("space", 1),), 2)
        else:
            padded = with_upwind_halo(distribution_table, signs)
        advected_distribution = transport(padded, along_x_part, along_y_part)
        distribution_table, kelvin_level = approach_increment(
            advected_distribution, site_kind, along_x_part, along_y_part, along_z_part
        )
    return (distribution_table, kelvin_level)


def solution(mesh):
    return jax.shard_map(
        per_device,
        mesh=mesh,
        in_specs=(P("vel", "space", None), P("space", None)),
        out_specs=(P("vel", "space", None), P("space", None)),
        check_vma=False,
    )
```

```python
import math

import jax
import numpy as np
import jax.numpy as jnp
from jax import lax
from jax.sharding import PartitionSpec as P


NVX = 24
STEPS = 2


speed_limit = 4.0
courant = 0.1
diffusivity_ratio = 2.0 / 3.0
power_law_index = 0.81
encounter_rate = 0.25
wall_kelvin = 1.0
inflow_concentration = 1.0
inflow_speed = 0.5
inflow_kelvin = 1.0


def with_halo(block, sides, width):
    for axis, dim in sides:
        count = lax.axis_size(axis)
        forward = [(i, i + 1) for i in range(count - 1)]
        backward = [(target, source) for source, target in forward]
        low = lax.ppermute(
            lax.slice_in_dim(block, block.shape[dim] - width, None, axis=dim), axis, forward
        )
        high = lax.ppermute(lax.slice_in_dim(block, 0, width, axis=dim), axis, backward)
        block = jnp.concatenate([low, block, high], axis=dim)
    return block


def halo_signs(vel_count, amount):
    spacing = 2.0 * speed_limit / (NVX - 1)
    signs = []
    for member in range(vel_count):
        index = np.arange(member * amount, (member + 1) * amount)
        along_x_part = np.float32(-speed_limit) + np.float32(spacing) * (index // (NVX * NVX)).astype(np.float32)
        if np.all(along_x_part > 0):
            signs.append(1)
        elif np.all(along_x_part < 0):
            signs.append(-1)
        else:
            return None
    return signs


def with_upwind_halo(block, signs):
    count = lax.axis_size("space")
    rows = block.shape[1]
    forward = [(i, i + 1) for i in range(count - 1)]
    backward = [(target, source) for source, target in forward]
    low = lax.ppermute(block[:, rows - 1 :], "space", forward)
    high = lax.ppermute(block[:, :1], "space", backward)
    pairs = []
    for member, sign in enumerate(signs):
        for source, target in forward if sign > 0 else backward:
            pairs.append((member * count + source, member * count + target))
    positive = jnp.asarray(np.array(signs, np.int32))[lax.axis_index("vel")] > 0
    extra = lax.ppermute(
        jnp.where(positive, block[:, rows - 2 : rows - 1], block[:, 1:2]), ("vel", "space"), pairs
    )
    return jnp.concatenate([extra, low, block, high, extra], axis=1)


def speeds(offset, amount):
    index = offset + jnp.arange(amount, dtype=jnp.int32)
    spacing = 2.0 * speed_limit / (NVX - 1)
    along_x_part = -speed_limit + spacing * (index // (NVX * NVX)).astype(jnp.float32)
    along_y_part = -speed_limit + spacing * (index // NVX % NVX).astype(jnp.float32)
    along_z_part = -speed_limit + spacing * (index % NVX).astype(jnp.float32)
    return (along_x_part, along_y_part, along_z_part)


def quad_weight():
    return (2.0 * speed_limit / (NVX - 1)) ** 3 / (2.0 * math.pi) ** 1.5


def minmod(left, right):
    return 0.5 * (jnp.sign(left) + jnp.sign(right)) * jnp.minimum(jnp.abs(left), jnp.abs(right))


def sweep(distribution_table, number, along):
    length = distribution_table.shape[along]

    def piece(source, low, high):
        return lax.slice_in_dim(source, low, high, axis=along)

    jumps = piece(distribution_table, 1, length) - piece(distribution_table, 0, length - 1)
    slopes = minmod(piece(jumps, 0, length - 2), piece(jumps, 1, length - 1))
    left_face = piece(distribution_table, 1, length - 2) + 0.5 * (1.0 - number) * piece(
        slopes, 0, length - 3
    )
    right_face = piece(distribution_table, 2, length - 1) - 0.5 * (1.0 + number) * piece(
        slopes, 1, length - 2
    )
    flux = number * jnp.where(number > 0, left_face, right_face)
    return piece(distribution_table, 2, length - 2) - (
        piece(flux, 1, length - 3) - piece(flux, 0, length - 4)
    )


def transport(padded, along_x_part, along_y_part):
    swept = sweep(padded, courant * along_x_part[:, None, None], 1)
    widened = jnp.pad(swept, ((0, 0), (0, 0), (2, 2)))
    return sweep(widened, courant * along_y_part[:, None, None], 2)


def xor_tree(values):
    while len(values) > 1:
        values = [values[2 * j] + values[2 * j + 1] for j in range(len(values) // 2)]
    return values[0]


def vel_sum(local):
    count = lax.axis_size("vel")
    if count & (count - 1):
        return lax.psum(local, "vel")
    bits = count.bit_length() - 1
    low = 0
    while low < bits:
        width = min(2, bits - low)
        values = [local]
        for member in range(1, 1 << width):
            mask = member << low
            values.append(lax.ppermute(local, "vel", [(i, i ^ mask) for i in range(count)]))
        local = xor_tree(values)
        low += width
    return local


def moment_totals(advected_distribution, along_x_part, along_y_part, along_z_part):
    magnitude_squares = (
        along_x_part * along_x_part + along_y_part * along_y_part + along_z_part * along_z_part
    )
    ones = jnp.ones_like(along_x_part)
    table = quad_weight() * jnp.stack(
        [
            ones,
            along_x_part,
            along_y_part,
            along_z_part,
            magnitude_squares,
            along_x_part * along_x_part,
            along_y_part * along_y_part,
            along_z_part * along_z_part,
            along_x_part * along_y_part,
            along_x_part * along_z_part,
            along_y_part * along_z_part,
            along_x_part * magnitude_squares,
            along_y_part * magnitude_squares,
            along_z_part * magnitude_squares,
            jnp.zeros_like(along_x_part),
            jnp.zeros_like(along_x_part),
        ]
    )
    local = jnp.einsum("kv,vrc->krc", table, advected_distribution, precision=lax.Precision.HIGHEST)
    return vel_sum(local)


def derived_moments(totals):
    particle_concentration = totals[0]
    average_drift_x = totals[1] / particle_concentration
    average_drift_y = totals[2] / particle_concentration
    average_drift_z = totals[3] / particle_concentration
    energy = totals[4]
    drift_square = (
        average_drift_x * average_drift_x
        + average_drift_y * average_drift_y
        + average_drift_z * average_drift_z
    )
    kelvin_level = (energy / particle_concentration - drift_square) / 3.0
    xx, yy, zz, xy, xz, yz = (totals[k] for k in range(5, 11))
    drift = (average_drift_x, average_drift_y, average_drift_z)
    second = ((xx, xy, xz), (xy, yy, yz), (xz, yz, zz))
    common = 2.0 * particle_concentration * drift_square
    conductive_transfer = jnp.stack(
        [
            0.5
            * (
                totals[11 + i]
                - 2.0 * (drift[0] * second[i][0] + drift[1] * second[i][1] + drift[2] * second[i][2])
                - drift[i] * energy
                + drift[i] * common
            )
            for i in range(3)
        ]
    )
    return (
        particle_concentration,
        average_drift_x,
        average_drift_y,
        average_drift_z,
        kelvin_level,
        conductive_transfer,
    )


def approach_increment(
    advected_distribution, kind_labels, along_x_part, along_y_part, along_z_part, totals
):
    (
        particle_concentration,
        average_drift_x,
        average_drift_y,
        average_drift_z,
        kelvin_level,
        conductive_transfer,
    ) = derived_moments(totals)
    rel_x = along_x_part[:, None, None] - average_drift_x[None]
    rel_y = along_y_part[:, None, None] - average_drift_y[None]
    rel_z = along_z_part[:, None, None] - average_drift_z[None]
    relative_magnitude_square = rel_x * rel_x + rel_y * rel_y + rel_z * rel_z
    stress_scalar_grid = particle_concentration * kelvin_level
    gaussian_local_balance = (
        particle_concentration
        * kelvin_level ** (-1.5)
        * jnp.exp(-relative_magnitude_square / (2.0 * kelvin_level))
    )
    conductive_vector_slot = (
        rel_x * conductive_transfer[0]
        + rel_y * conductive_transfer[1]
        + rel_z * conductive_transfer[2]
    )
    corrected_goal_distribution = gaussian_local_balance * (
        1.0
        + (1.0 - diffusivity_ratio)
        * conductive_vector_slot
        * (relative_magnitude_square / kelvin_level - 5.0)
        / (5.0 * stress_scalar_grid * kelvin_level)
    )
    approach_rate = (
        encounter_rate * particle_concentration * kelvin_level ** (1.0 - power_law_index)
    )
    relaxed = advected_distribution + approach_rate * (
        corrected_goal_distribution - advected_distribution
    )
    magnitude_squares = (
        along_x_part * along_x_part + along_y_part * along_y_part + along_z_part * along_z_part
    )[:, None, None]
    wall_distribution = (
        particle_concentration
        * wall_kelvin ** (-1.5)
        * jnp.exp(-magnitude_squares / (2.0 * wall_kelvin))
    )
    inflow_magnitude_square = (
        (along_x_part - inflow_speed) ** 2
        + along_y_part * along_y_part
        + along_z_part * along_z_part
    )[:, None, None]
    inflow_distribution = (
        inflow_concentration
        * inflow_kelvin ** (-1.5)
        * jnp.exp(-inflow_magnitude_square / (2.0 * inflow_kelvin))
    )
    revised_distribution = jnp.where(
        kind_labels == 1,
        wall_distribution,
        jnp.where(kind_labels == 2, inflow_distribution, relaxed),
    )
    return (revised_distribution, kelvin_level)


def per_device(initial, site_kind):
    amount = initial.shape[0]
    along_x_part, along_y_part, along_z_part = speeds(lax.axis_index("vel") * amount, amount)
    distribution_table = initial
    kelvin_level = jnp.zeros(site_kind.shape, jnp.float32)
    rows = distribution_table.shape[1]
    signs = halo_signs(lax.axis_size("vel"), amount)
    if signs is None or rows < 2:
        for _ in range(STEPS):
            padded = with_halo(distribution_table, (("space", 1),), 2)
            advected_distribution = transport(padded, along_x_part, along_y_part)
            totals = moment_totals(advected_distribution, along_x_part, along_y_part, along_z_part)
            distribution_table, kelvin_level = approach_increment(
                advected_distribution, site_kind, along_x_part, along_y_part, along_z_part, totals
            )
        return (distribution_table, kelvin_level)
    count = lax.axis_size("space")
    place = lax.axis_index("space") * rows + jnp.arange(rows + 4) - 2
    positive = jnp.asarray(np.array(signs, np.int32))[lax.axis_index("vel")] > 0
    slot = jnp.arange(rows + 4)
    keep = (place >= 0) & (place < count * rows)
    keep = keep & jnp.where(positive, slot != rows + 3, slot != 0)
    padded_kinds = with_upwind_halo(site_kind.astype(jnp.float32)[None], signs)[0]
    padded = with_upwind_halo(distribution_table, signs)
    for section in range(STEPS):
        distribution_table, kelvin_level, padded = upwind_step(
            section, padded, padded_kinds, keep, site_kind, signs, along_x_part, along_y_part, along_z_part
        )
    return (distribution_table, kelvin_level)


def upwind_step(section, padded, padded_kinds, keep, site_kind, signs, along_x_part, along_y_part, along_z_part):
    distribution_table = kelvin_level = None
    advected_distribution = transport(padded, along_x_part, along_y_part)
    if section + 1 < STEPS:
        advected_padded = with_upwind_halo(advected_distribution, signs)
    totals = moment_totals(advected_distribution, along_x_part, along_y_part, along_z_part)
    if section + 1 < STEPS:
        revised, _ = approach_increment(
            advected_padded,
            padded_kinds.astype(jnp.int32),
            along_x_part,
            along_y_part,
            along_z_part,
            with_upwind_halo(totals, signs),
        )
        padded = jnp.where(keep[None, :, None], revised, 0.0)
    else:
        distribution_table, kelvin_level = approach_increment(
            advected_distribution, site_kind, along_x_part, along_y_part, along_z_part, totals
        )
    return distribution_table, kelvin_level, padded


def solution(mesh):
    return jax.shard_map(
        per_device,
        mesh=mesh,
        in_specs=(P("vel", "space", None), P("space", None)),
        out_specs=(P("vel", "space", None), P("space", None)),
        check_vma=False,
    )
```

```python
import math

import jax
import numpy as np
import jax.numpy as jnp
from jax import lax
from jax.sharding import PartitionSpec as P

NVX = 24
STEPS = 2


speed_limit = 4.0
courant = 0.1
diffusivity_ratio = 2.0 / 3.0
power_law_index = 0.81
encounter_rate = 0.25
wall_kelvin = 1.0
inflow_concentration = 1.0
inflow_speed = 0.5
inflow_kelvin = 1.0


def with_halo(block, sides, width):
    for axis, dim in sides:
        count = lax.axis_size(axis)
        forward = [(i, i + 1) for i in range(count - 1)]
        backward = [(target, source) for source, target in forward]
        low = lax.ppermute(
            lax.slice_in_dim(block, block.shape[dim] - width, None, axis=dim), axis, forward
        )
        high = lax.ppermute(lax.slice_in_dim(block, 0, width, axis=dim), axis, backward)
        block = jnp.concatenate([low, block, high], axis=dim)
    return block


def halo_signs(vel_count, amount):
    spacing = 2.0 * speed_limit / (NVX - 1)
    signs = []
    for member in range(vel_count):
        index = np.arange(member * amount, (member + 1) * amount)
        along_x_part = np.float32(-speed_limit) + np.float32(spacing) * (index // (NVX * NVX)).astype(np.float32)
        if np.all(along_x_part > 0):
            signs.append(1)
        elif np.all(along_x_part < 0):
            signs.append(-1)
        else:
            return None
    return signs


def with_upwind_halo(block, signs):
    count = lax.axis_size("space")
    rows = block.shape[1]
    forward = [(i, i + 1) for i in range(count - 1)]
    backward = [(target, source) for source, target in forward]
    upwind = []
    downwind = []
    for member, sign in enumerate(signs):
        for source, target in forward:
            pair = (member * count + source, member * count + target)
            (upwind if sign > 0 else downwind).append(pair)
        for source, target in backward:
            pair = (member * count + source, member * count + target)
            (downwind if sign > 0 else upwind).append(pair)
    positive = jnp.asarray(np.array(signs, np.int32))[lax.axis_index("vel")] > 0
    wide = lax.ppermute(
        jnp.where(positive, block[:, rows - 2 :], block[:, :2]), ("vel", "space"), upwind
    )
    narrow = lax.ppermute(
        jnp.where(positive, block[:, :1], block[:, rows - 1 :]), ("vel", "space"), downwind
    )
    low = jnp.where(positive, wide, jnp.concatenate([narrow, narrow], axis=1))
    high = jnp.where(positive, jnp.concatenate([narrow, narrow], axis=1), wide)
    return jnp.concatenate([low, block, high], axis=1)


def speeds(offset, amount):
    index = offset + jnp.arange(amount, dtype=jnp.int32)
    spacing = 2.0 * speed_limit / (NVX - 1)
    along_x_part = -speed_limit + spacing * (index // (NVX * NVX)).astype(jnp.float32)
    along_y_part = -speed_limit + spacing * (index // NVX % NVX).astype(jnp.float32)
    along_z_part = -speed_limit + spacing * (index % NVX).astype(jnp.float32)
    return (along_x_part, along_y_part, along_z_part)


def quad_weight():
    return (2.0 * speed_limit / (NVX - 1)) ** 3 / (2.0 * math.pi) ** 1.5


def minmod(left, right):
    return 0.5 * (jnp.sign(left) + jnp.sign(right)) * jnp.minimum(jnp.abs(left), jnp.abs(right))


def sweep(distribution_table, number, along):
    length = distribution_table.shape[along]

    def piece(source, low, high):
        return lax.slice_in_dim(source, low, high, axis=along)

    jumps = piece(distribution_table, 1, length) - piece(distribution_table, 0, length - 1)
    slopes = minmod(piece(jumps, 0, length - 2), piece(jumps, 1, length - 1))
    left_face = piece(distribution_table, 1, length - 2) + 0.5 * (1.0 - number) * piece(
        slopes, 0, length - 3
    )
    right_face = piece(distribution_table, 2, length - 1) - 0.5 * (1.0 + number) * piece(
        slopes, 1, length - 2
    )
    flux = number * jnp.where(number > 0, left_face, right_face)
    return piece(distribution_table, 2, length - 2) - (
        piece(flux, 1, length - 3) - piece(flux, 0, length - 4)
    )


def transport(padded, along_x_part, along_y_part):
    swept = sweep(padded, courant * along_x_part[:, None, None], 1)
    widened = jnp.pad(swept, ((0, 0), (0, 0), (2, 2)))
    return sweep(widened, courant * along_y_part[:, None, None], 2)


def xor_tree(values):
    while len(values) > 1:
        values = [values[2 * j] + values[2 * j + 1] for j in range(len(values) // 2)]
    return values[0]


def vel_sum(local):
    count = lax.axis_size("vel")
    if count & (count - 1):
        return lax.psum(local, "vel")
    bits = count.bit_length() - 1
    low = 0
    while low < bits:
        width = min(2, bits - low)
        values = [local]
        for member in range(1, 1 << width):
            mask = member << low
            values.append(lax.ppermute(local, "vel", [(i, i ^ mask) for i in range(count)]))
        local = xor_tree(values)
        low += width
    return local


def macroscopic_moments(advected_distribution, along_x_part, along_y_part, along_z_part):
    magnitude_squares = (
        along_x_part * along_x_part + along_y_part * along_y_part + along_z_part * along_z_part
    )
    ones = jnp.ones_like(along_x_part)
    table = quad_weight() * jnp.stack(
        [
            ones,
            along_x_part,
            along_y_part,
            along_z_part,
            magnitude_squares,
            along_x_part * along_x_part,
            along_y_part * along_y_part,
            along_z_part * along_z_part,
            along_x_part * along_y_part,
            along_x_part * along_z_part,
            along_y_part * along_z_part,
            along_x_part * magnitude_squares,
            along_y_part * magnitude_squares,
            along_z_part * magnitude_squares,
            jnp.zeros_like(along_x_part),
            jnp.zeros_like(along_x_part),
        ]
    )
    local = jnp.einsum("kv,vrc->krc", table, advected_distribution, precision=lax.Precision.HIGHEST)
    totals = vel_sum(local)
    particle_concentration = totals[0]
    average_drift_x = totals[1] / particle_concentration
    average_drift_y = totals[2] / particle_concentration
    average_drift_z = totals[3] / particle_concentration
    energy = totals[4]
    drift_square = (
        average_drift_x * average_drift_x
        + average_drift_y * average_drift_y
        + average_drift_z * average_drift_z
    )
    kelvin_level = (energy / particle_concentration - drift_square) / 3.0
    xx, yy, zz, xy, xz, yz = (totals[k] for k in range(5, 11))
    drift = (average_drift_x, average_drift_y, average_drift_z)
    second = ((xx, xy, xz), (xy, yy, yz), (xz, yz, zz))
    common = 2.0 * particle_concentration * drift_square
    conductive_transfer = jnp.stack(
        [
            0.5
            * (
                totals[11 + i]
                - 2.0 * (drift[0] * second[i][0] + drift[1] * second[i][1] + drift[2] * second[i][2])
                - drift[i] * energy
                + drift[i] * common
            )
            for i in range(3)
        ]
    )
    return (
        particle_concentration,
        average_drift_x,
        average_drift_y,
        average_drift_z,
        kelvin_level,
        conductive_transfer,
    )


def approach_increment(
    advected_distribution, kind_labels, along_x_part, along_y_part, along_z_part
):
    (
        particle_concentration,
        average_drift_x,
        average_drift_y,
        average_drift_z,
        kelvin_level,
        conductive_transfer,
    ) = macroscopic_moments(advected_distribution, along_x_part, along_y_part, along_z_part)
    rel_x = along_x_part[:, None, None] - average_drift_x[None]
    rel_y = along_y_part[:, None, None] - average_drift_y[None]
    rel_z = along_z_part[:, None, None] - average_drift_z[None]
    relative_magnitude_square = rel_x * rel_x + rel_y * rel_y + rel_z * rel_z
    stress_scalar_grid = particle_concentration * kelvin_level
    gaussian_local_balance = (
        particle_concentration
        * kelvin_level ** (-1.5)
        * jnp.exp(-relative_magnitude_square / (2.0 * kelvin_level))
    )
    conductive_vector_slot = (
        rel_x * conductive_transfer[0]
        + rel_y * conductive_transfer[1]
        + rel_z * conductive_transfer[2]
    )
    corrected_goal_distribution = gaussian_local_balance * (
        1.0
        + (1.0 - diffusivity_ratio)
        * conductive_vector_slot
        * (relative_magnitude_square / kelvin_level - 5.0)
        / (5.0 * stress_scalar_grid * kelvin_level)
    )
    approach_rate = (
        encounter_rate * particle_concentration * kelvin_level ** (1.0 - power_law_index)
    )
    relaxed = advected_distribution + approach_rate * (
        corrected_goal_distribution - advected_distribution
    )
    magnitude_squares = (
        along_x_part * along_x_part + along_y_part * along_y_part + along_z_part * along_z_part
    )[:, None, None]
    wall_distribution = (
        particle_concentration
        * wall_kelvin ** (-1.5)
        * jnp.exp(-magnitude_squares / (2.0 * wall_kelvin))
    )
    inflow_magnitude_square = (
        (along_x_part - inflow_speed) ** 2
        + along_y_part * along_y_part
        + along_z_part * along_z_part
    )[:, None, None]
    inflow_distribution = (
        inflow_concentration
        * inflow_kelvin ** (-1.5)
        * jnp.exp(-inflow_magnitude_square / (2.0 * inflow_kelvin))
    )
    revised_distribution = jnp.where(
        kind_labels == 1,
        wall_distribution,
        jnp.where(kind_labels == 2, inflow_distribution, relaxed),
    )
    return (revised_distribution, kelvin_level)


def per_device(initial, site_kind):
    amount = initial.shape[0]
    along_x_part, along_y_part, along_z_part = speeds(lax.axis_index("vel") * amount, amount)
    distribution_table = initial
    kelvin_level = jnp.zeros(site_kind.shape, jnp.float32)
    signs = halo_signs(lax.axis_size("vel"), amount)
    for section in range(STEPS):
        if signs is None or distribution_table.shape[1] < 2:
            padded = with_halo(distribution_table, (("space", 1),), 2)
        else:
            padded = with_upwind_halo(distribution_table, signs)
        advected_distribution = transport(padded, along_x_part, along_y_part)
        distribution_table, kelvin_level = approach_increment(
            advected_distribution, site_kind, along_x_part, along_y_part, along_z_part
        )
    return (distribution_table, kelvin_level)


def solution(mesh):
    return jax.shard_map(
        per_device,
        mesh=mesh,
        in_specs=(P("vel", "space", None), P("space", None)),
        out_specs=(P("vel", "space", None), P("space", None)),
        check_vma=False,
    )
```

```python
import math
import os

import jax
import numpy as np
import jax.numpy as jnp
from jax import lax
from jax.experimental import pallas as pl
from jax.experimental.pallas import tpu as pltpu
from jax.sharding import PartitionSpec as P

NVX = 24
STEPS = 2


speed_limit = 4.0
courant = 0.1
diffusivity_ratio = 2.0 / 3.0
power_law_index = 0.81
encounter_rate = 0.25
wall_kelvin = 1.0
inflow_concentration = 1.0
inflow_speed = 0.5
inflow_kelvin = 1.0


def with_halo(block, sides, width):
    for axis, dim in sides:
        count = lax.axis_size(axis)
        forward = [(i, i + 1) for i in range(count - 1)]
        backward = [(target, source) for source, target in forward]
        low = lax.ppermute(
            lax.slice_in_dim(block, block.shape[dim] - width, None, axis=dim), axis, forward
        )
        high = lax.ppermute(lax.slice_in_dim(block, 0, width, axis=dim), axis, backward)
        block = jnp.concatenate([low, block, high], axis=dim)
    return block


def halo_signs(vel_count, amount):
    spacing = 2.0 * speed_limit / (NVX - 1)
    signs = []
    for member in range(vel_count):
        index = np.arange(member * amount, (member + 1) * amount)
        along_x_part = np.float32(-speed_limit) + np.float32(spacing) * (index // (NVX * NVX)).astype(np.float32)
        if np.all(along_x_part > 0):
            signs.append(1)
        elif np.all(along_x_part < 0):
            signs.append(-1)
        else:
            return None
    return signs


def with_upwind_halo(block, signs):
    count = lax.axis_size("space")
    rows = block.shape[1]
    forward = [(i, i + 1) for i in range(count - 1)]
    backward = [(target, source) for source, target in forward]
    low = lax.ppermute(block[:, rows - 1 :], "space", forward)
    high = lax.ppermute(block[:, :1], "space", backward)
    pairs = []
    for member, sign in enumerate(signs):
        for source, target in forward if sign > 0 else backward:
            pairs.append((member * count + source, member * count + target))
    positive = jnp.asarray(np.array(signs, np.int32))[lax.axis_index("vel")] > 0
    extra = lax.ppermute(
        jnp.where(positive, block[:, rows - 2 : rows - 1], block[:, 1:2]), ("vel", "space"), pairs
    )
    return jnp.concatenate([extra, low, block, high, extra], axis=1)


def speeds(offset, amount):
    index = offset + jnp.arange(amount, dtype=jnp.int32)
    spacing = 2.0 * speed_limit / (NVX - 1)
    along_x_part = -speed_limit + spacing * (index // (NVX * NVX)).astype(jnp.float32)
    along_y_part = -speed_limit + spacing * (index // NVX % NVX).astype(jnp.float32)
    along_z_part = -speed_limit + spacing * (index % NVX).astype(jnp.float32)
    return (along_x_part, along_y_part, along_z_part)


def quad_weight():
    return (2.0 * speed_limit / (NVX - 1)) ** 3 / (2.0 * math.pi) ** 1.5


def minmod(left, right):
    return 0.5 * (jnp.sign(left) + jnp.sign(right)) * jnp.minimum(jnp.abs(left), jnp.abs(right))


def sweep(distribution_table, number, along):
    length = distribution_table.shape[along]

    def piece(source, low, high):
        return lax.slice_in_dim(source, low, high, axis=along)

    jumps = piece(distribution_table, 1, length) - piece(distribution_table, 0, length - 1)
    slopes = minmod(piece(jumps, 0, length - 2), piece(jumps, 1, length - 1))
    left_face = piece(distribution_table, 1, length - 2) + 0.5 * (1.0 - number) * piece(
        slopes, 0, length - 3
    )
    right_face = piece(distribution_table, 2, length - 1) - 0.5 * (1.0 + number) * piece(
        slopes, 1, length - 2
    )
    flux = number * jnp.where(number > 0, left_face, right_face)
    return piece(distribution_table, 2, length - 2) - (
        piece(flux, 1, length - 3) - piece(flux, 0, length - 4)
    )


def kernel_minmod(left, right):
    both_up = (left > 0) & (right > 0)
    both_down = (left < 0) & (right < 0)
    return jnp.where(
        both_up, jnp.minimum(left, right), jnp.where(both_down, jnp.maximum(left, right), 0.0)
    )


def face_flux(number, lower, upper, lower_slope, upper_slope):
    return number * jnp.where(
        number > 0,
        lower + 0.5 * (1.0 - number) * lower_slope,
        upper - 0.5 * (1.0 + number) * upper_slope,
    )


def transport_kernel(number_x_ref, number_y_ref, padded_ref, out_ref):
    number_x = number_x_ref[...]
    number_y = number_y_ref[...]
    depth = padded_ref.shape[0]
    values = [padded_ref[k] for k in range(depth)]
    jumps = [values[k + 1] - values[k] for k in range(depth - 1)]
    slopes = {k: kernel_minmod(jumps[k - 1], jumps[k]) for k in range(1, depth - 1)}
    flux = {
        k: face_flux(number_x, values[k], values[k + 1], slopes[k], slopes[k + 1])
        for k in range(1, depth - 2)
    }
    width = values[0].shape[-1]
    lane = lax.broadcasted_iota(jnp.int32, values[0].shape, 1)
    first = lane == 0
    last = lane == width - 1
    for k in range(2, depth - 2):
        swept = values[k] - (flux[k] - flux[k - 1])
        before = jnp.where(first, 0.0, pltpu.roll(swept, 1, 1))
        after = jnp.where(last, 0.0, pltpu.roll(swept, width - 1, 1))
        slope = kernel_minmod(swept - before, after - swept)
        slope_before = jnp.where(first, 0.0, pltpu.roll(slope, 1, 1))
        slope_after = jnp.where(last, 0.0, pltpu.roll(slope, width - 1, 1))
        flux_after = face_flux(number_y, swept, after, slope, slope_after)
        flux_before = face_flux(number_y, before, swept, slope_before, slope)
        out_ref[k - 2] = swept - (flux_after - flux_before)


def transport(padded, along_x_part, along_y_part):
    amount, depth, width = padded.shape
    rows = depth - 4
    block = 96 if amount % 96 == 0 else amount
    number_x = (courant * along_x_part)[:, None]
    number_y = (courant * along_y_part)[:, None]
    stacked = jnp.transpose(padded, (1, 0, 2))
    swept = pl.pallas_call(
        transport_kernel,
        grid=(amount // block,),
        in_specs=[
            pl.BlockSpec((block, 1), lambda i: (i, 0)),
            pl.BlockSpec((block, 1), lambda i: (i, 0)),
            pl.BlockSpec((depth, block, width), lambda i: (0, i, 0)),
        ],
        out_specs=pl.BlockSpec((rows, block, width), lambda i: (0, i, 0)),
        out_shape=jax.ShapeDtypeStruct((rows, amount, width), padded.dtype),
        interpret=os.environ.get("SOLUTION_INTERPRET") == "1",
    )(number_x, number_y, stacked)
    return jnp.transpose(swept, (1, 0, 2))


def xor_tree(values):
    while len(values) > 1:
        values = [values[2 * j] + values[2 * j + 1] for j in range(len(values) // 2)]
    return values[0]


def vel_sum(local):
    count = lax.axis_size("vel")
    if count & (count - 1):
        return lax.psum(local, "vel")
    bits = count.bit_length() - 1
    low = 0
    while low < bits:
        width = min(2, bits - low)
        values = [local]
        for member in range(1, 1 << width):
            mask = member << low
            values.append(lax.ppermute(local, "vel", [(i, i ^ mask) for i in range(count)]))
        local = xor_tree(values)
        low += width
    return local


def macroscopic_moments(advected_distribution, along_x_part, along_y_part, along_z_part):
    magnitude_squares = (
        along_x_part * along_x_part + along_y_part * along_y_part + along_z_part * along_z_part
    )
    ones = jnp.ones_like(along_x_part)
    table = quad_weight() * jnp.stack(
        [
            ones,
            along_x_part,
            along_y_part,
            along_z_part,
            magnitude_squares,
            along_x_part * along_x_part,
            along_y_part * along_y_part,
            along_z_part * along_z_part,
            along_x_part * along_y_part,
            along_x_part * along_z_part,
            along_y_part * along_z_part,
            along_x_part * magnitude_squares,
            along_y_part * magnitude_squares,
            along_z_part * magnitude_squares,
            jnp.zeros_like(along_x_part),
            jnp.zeros_like(along_x_part),
        ]
    )
    local = jnp.einsum("kv,vrc->krc", table, advected_distribution, precision=lax.Precision.HIGHEST)
    totals = vel_sum(local)
    particle_concentration = totals[0]
    average_drift_x = totals[1] / particle_concentration
    average_drift_y = totals[2] / particle_concentration
    average_drift_z = totals[3] / particle_concentration
    energy = totals[4]
    drift_square = (
        average_drift_x * average_drift_x
        + average_drift_y * average_drift_y
        + average_drift_z * average_drift_z
    )
    kelvin_level = (energy / particle_concentration - drift_square) / 3.0
    xx, yy, zz, xy, xz, yz = (totals[k] for k in range(5, 11))
    drift = (average_drift_x, average_drift_y, average_drift_z)
    second = ((xx, xy, xz), (xy, yy, yz), (xz, yz, zz))
    common = 2.0 * particle_concentration * drift_square
    conductive_transfer = jnp.stack(
        [
            0.5
            * (
                totals[11 + i]
                - 2.0 * (drift[0] * second[i][0] + drift[1] * second[i][1] + drift[2] * second[i][2])
                - drift[i] * energy
                + drift[i] * common
            )
            for i in range(3)
        ]
    )
    return (
        particle_concentration,
        average_drift_x,
        average_drift_y,
        average_drift_z,
        kelvin_level,
        conductive_transfer,
    )


def approach_increment(
    advected_distribution, kind_labels, along_x_part, along_y_part, along_z_part
):
    (
        particle_concentration,
        average_drift_x,
        average_drift_y,
        average_drift_z,
        kelvin_level,
        conductive_transfer,
    ) = macroscopic_moments(advected_distribution, along_x_part, along_y_part, along_z_part)
    rel_x = along_x_part[:, None, None] - average_drift_x[None]
    rel_y = along_y_part[:, None, None] - average_drift_y[None]
    rel_z = along_z_part[:, None, None] - average_drift_z[None]
    relative_magnitude_square = rel_x * rel_x + rel_y * rel_y + rel_z * rel_z
    stress_scalar_grid = particle_concentration * kelvin_level
    gaussian_local_balance = (
        particle_concentration
        * kelvin_level ** (-1.5)
        * jnp.exp(-relative_magnitude_square / (2.0 * kelvin_level))
    )
    conductive_vector_slot = (
        rel_x * conductive_transfer[0]
        + rel_y * conductive_transfer[1]
        + rel_z * conductive_transfer[2]
    )
    corrected_goal_distribution = gaussian_local_balance * (
        1.0
        + (1.0 - diffusivity_ratio)
        * conductive_vector_slot
        * (relative_magnitude_square / kelvin_level - 5.0)
        / (5.0 * stress_scalar_grid * kelvin_level)
    )
    approach_rate = (
        encounter_rate * particle_concentration * kelvin_level ** (1.0 - power_law_index)
    )
    relaxed = advected_distribution + approach_rate * (
        corrected_goal_distribution - advected_distribution
    )
    magnitude_squares = (
        along_x_part * along_x_part + along_y_part * along_y_part + along_z_part * along_z_part
    )[:, None, None]
    wall_distribution = (
        particle_concentration
        * wall_kelvin ** (-1.5)
        * jnp.exp(-magnitude_squares / (2.0 * wall_kelvin))
    )
    inflow_magnitude_square = (
        (along_x_part - inflow_speed) ** 2
        + along_y_part * along_y_part
        + along_z_part * along_z_part
    )[:, None, None]
    inflow_distribution = (
        inflow_concentration
        * inflow_kelvin ** (-1.5)
        * jnp.exp(-inflow_magnitude_square / (2.0 * inflow_kelvin))
    )
    revised_distribution = jnp.where(
        kind_labels == 1,
        wall_distribution,
        jnp.where(kind_labels == 2, inflow_distribution, relaxed),
    )
    return (revised_distribution, kelvin_level)


def per_device(initial, site_kind):
    amount = initial.shape[0]
    along_x_part, along_y_part, along_z_part = speeds(lax.axis_index("vel") * amount, amount)
    distribution_table = initial
    kelvin_level = jnp.zeros(site_kind.shape, jnp.float32)
    signs = halo_signs(lax.axis_size("vel"), amount)
    for section in range(STEPS):
        if signs is None or distribution_table.shape[1] < 2:
            padded = with_halo(distribution_table, (("space", 1),), 2)
        else:
            padded = with_upwind_halo(distribution_table, signs)
        advected_distribution = transport(padded, along_x_part, along_y_part)
        distribution_table, kelvin_level = approach_increment(
            advected_distribution, site_kind, along_x_part, along_y_part, along_z_part
        )
    return (distribution_table, kelvin_level)


def solution(mesh):
    return jax.shard_map(
        per_device,
        mesh=mesh,
        in_specs=(P("vel", "space", None), P("space", None)),
        out_specs=(P("vel", "space", None), P("space", None)),
        check_vma=False,
    )
```

```python
import math

import jax
import numpy as np
import jax.numpy as jnp
from jax import lax
from jax.sharding import PartitionSpec as P

NVX = 24
STEPS = 2


speed_limit = 4.0
courant = 0.1
diffusivity_ratio = 2.0 / 3.0
power_law_index = 0.81
encounter_rate = 0.25
wall_kelvin = 1.0
inflow_concentration = 1.0
inflow_speed = 0.5
inflow_kelvin = 1.0


def with_halo(block, sides, width):
    for axis, dim in sides:
        count = lax.axis_size(axis)
        forward = [(i, i + 1) for i in range(count - 1)]
        backward = [(target, source) for source, target in forward]
        low = lax.ppermute(
            lax.slice_in_dim(block, block.shape[dim] - width, None, axis=dim), axis, forward
        )
        high = lax.ppermute(lax.slice_in_dim(block, 0, width, axis=dim), axis, backward)
        block = jnp.concatenate([low, block, high], axis=dim)
    return block


def halo_signs(vel_count, amount):
    spacing = 2.0 * speed_limit / (NVX - 1)
    signs = []
    for member in range(vel_count):
        index = np.arange(member * amount, (member + 1) * amount)
        along_x_part = np.float32(-speed_limit) + np.float32(spacing) * (index // (NVX * NVX)).astype(np.float32)
        if np.all(along_x_part > 0):
            signs.append(1)
        elif np.all(along_x_part < 0):
            signs.append(-1)
        else:
            return None
    return signs


def with_upwind_halo(block, signs):
    count = lax.axis_size("space")
    rows = block.shape[1]
    forward = [(i, i + 1) for i in range(count - 1)]
    backward = [(target, source) for source, target in forward]
    low = lax.ppermute(block[:, rows - 1 :], "space", forward)
    high = lax.ppermute(block[:, :1], "space", backward)
    pairs = []
    for member, sign in enumerate(signs):
        for source, target in forward if sign > 0 else backward:
            pairs.append((member * count + source, member * count + target))
    positive = jnp.asarray(np.array(signs, np.int32))[lax.axis_index("vel")] > 0
    extra = lax.ppermute(
        jnp.where(positive, block[:, rows - 2 : rows - 1], block[:, 1:2]), ("vel", "space"), pairs
    )
    return jnp.concatenate([extra, low, block, high, extra], axis=1)


def speeds(offset, amount):
    index = offset + jnp.arange(amount, dtype=jnp.int32)
    spacing = 2.0 * speed_limit / (NVX - 1)
    along_x_part = -speed_limit + spacing * (index // (NVX * NVX)).astype(jnp.float32)
    along_y_part = -speed_limit + spacing * (index // NVX % NVX).astype(jnp.float32)
    along_z_part = -speed_limit + spacing * (index % NVX).astype(jnp.float32)
    return (along_x_part, along_y_part, along_z_part)


def quad_weight():
    return (2.0 * speed_limit / (NVX - 1)) ** 3 / (2.0 * math.pi) ** 1.5


def minmod(left, right):
    return 0.5 * (jnp.sign(left) + jnp.sign(right)) * jnp.minimum(jnp.abs(left), jnp.abs(right))


def sweep(distribution_table, number, along):
    length = distribution_table.shape[along]

    def piece(source, low, high):
        return lax.slice_in_dim(source, low, high, axis=along)

    jumps = piece(distribution_table, 1, length) - piece(distribution_table, 0, length - 1)
    slopes = minmod(piece(jumps, 0, length - 2), piece(jumps, 1, length - 1))
    left_face = piece(distribution_table, 1, length - 2) + 0.5 * (1.0 - number) * piece(
        slopes, 0, length - 3
    )
    right_face = piece(distribution_table, 2, length - 1) - 0.5 * (1.0 + number) * piece(
        slopes, 1, length - 2
    )
    flux = number * jnp.where(number > 0, left_face, right_face)
    return piece(distribution_table, 2, length - 2) - (
        piece(flux, 1, length - 3) - piece(flux, 0, length - 4)
    )


def transport(padded, along_x_part, along_y_part):
    swept = sweep(padded, courant * along_x_part[:, None, None], 1)
    widened = jnp.pad(swept, ((0, 0), (0, 0), (2, 2)))
    return sweep(widened, courant * along_y_part[:, None, None], 2)


def xor_tree(values):
    while len(values) > 1:
        values = [values[2 * j] + values[2 * j + 1] for j in range(len(values) // 2)]
    return values[0]


def vel_sum(local):
    count = lax.axis_size("vel")
    if count & (count - 1):
        return lax.psum(local, "vel")
    bits = count.bit_length() - 1
    groups = []
    low = 0
    while low < bits:
        groups.append((low, min(2, bits - low)))
        low += 2
    for low, width in reversed(groups):
        values = [local]
        for member in range(1, 1 << width):
            mask = member << low
            values.append(lax.ppermute(local, "vel", [(i, i ^ mask) for i in range(count)]))
        local = xor_tree(values)
    return local


def macroscopic_moments(advected_distribution, along_x_part, along_y_part, along_z_part):
    magnitude_squares = (
        along_x_part * along_x_part + along_y_part * along_y_part + along_z_part * along_z_part
    )
    ones = jnp.ones_like(along_x_part)
    table = quad_weight() * jnp.stack(
        [
            ones,
            along_x_part,
            along_y_part,
            along_z_part,
            magnitude_squares,
            along_x_part * along_x_part,
            along_y_part * along_y_part,
            along_z_part * along_z_part,
            along_x_part * along_y_part,
            along_x_part * along_z_part,
            along_y_part * along_z_part,
            along_x_part * magnitude_squares,
            along_y_part * magnitude_squares,
            along_z_part * magnitude_squares,
            jnp.zeros_like(along_x_part),
            jnp.zeros_like(along_x_part),
        ]
    )
    local = jnp.einsum("kv,vrc->krc", table, advected_distribution, precision=lax.Precision.HIGHEST)
    totals = vel_sum(local)
    particle_concentration = totals[0]
    average_drift_x = totals[1] / particle_concentration
    average_drift_y = totals[2] / particle_concentration
    average_drift_z = totals[3] / particle_concentration
    energy = totals[4]
    drift_square = (
        average_drift_x * average_drift_x
        + average_drift_y * average_drift_y
        + average_drift_z * average_drift_z
    )
    kelvin_level = (energy / particle_concentration - drift_square) / 3.0
    xx, yy, zz, xy, xz, yz = (totals[k] for k in range(5, 11))
    drift = (average_drift_x, average_drift_y, average_drift_z)
    second = ((xx, xy, xz), (xy, yy, yz), (xz, yz, zz))
    common = 2.0 * particle_concentration * drift_square
    conductive_transfer = jnp.stack(
        [
            0.5
            * (
                totals[11 + i]
                - 2.0 * (drift[0] * second[i][0] + drift[1] * second[i][1] + drift[2] * second[i][2])
                - drift[i] * energy
                + drift[i] * common
            )
            for i in range(3)
        ]
    )
    return (
        particle_concentration,
        average_drift_x,
        average_drift_y,
        average_drift_z,
        kelvin_level,
        conductive_transfer,
    )


def approach_increment(
    advected_distribution, kind_labels, along_x_part, along_y_part, along_z_part
):
    (
        particle_concentration,
        average_drift_x,
        average_drift_y,
        average_drift_z,
        kelvin_level,
        conductive_transfer,
    ) = macroscopic_moments(advected_distribution, along_x_part, along_y_part, along_z_part)
    rel_x = along_x_part[:, None, None] - average_drift_x[None]
    rel_y = along_y_part[:, None, None] - average_drift_y[None]
    rel_z = along_z_part[:, None, None] - average_drift_z[None]
    relative_magnitude_square = rel_x * rel_x + rel_y * rel_y + rel_z * rel_z
    stress_scalar_grid = particle_concentration * kelvin_level
    gaussian_local_balance = (
        particle_concentration
        * kelvin_level ** (-1.5)
        * jnp.exp(-relative_magnitude_square / (2.0 * kelvin_level))
    )
    conductive_vector_slot = (
        rel_x * conductive_transfer[0]
        + rel_y * conductive_transfer[1]
        + rel_z * conductive_transfer[2]
    )
    corrected_goal_distribution = gaussian_local_balance * (
        1.0
        + (1.0 - diffusivity_ratio)
        * conductive_vector_slot
        * (relative_magnitude_square / kelvin_level - 5.0)
        / (5.0 * stress_scalar_grid * kelvin_level)
    )
    approach_rate = (
        encounter_rate * particle_concentration * kelvin_level ** (1.0 - power_law_index)
    )
    relaxed = advected_distribution + approach_rate * (
        corrected_goal_distribution - advected_distribution
    )
    magnitude_squares = (
        along_x_part * along_x_part + along_y_part * along_y_part + along_z_part * along_z_part
    )[:, None, None]
    wall_distribution = (
        particle_concentration
        * wall_kelvin ** (-1.5)
        * jnp.exp(-magnitude_squares / (2.0 * wall_kelvin))
    )
    inflow_magnitude_square = (
        (along_x_part - inflow_speed) ** 2
        + along_y_part * along_y_part
        + along_z_part * along_z_part
    )[:, None, None]
    inflow_distribution = (
        inflow_concentration
        * inflow_kelvin ** (-1.5)
        * jnp.exp(-inflow_magnitude_square / (2.0 * inflow_kelvin))
    )
    revised_distribution = jnp.where(
        kind_labels == 1,
        wall_distribution,
        jnp.where(kind_labels == 2, inflow_distribution, relaxed),
    )
    return (revised_distribution, kelvin_level)


def per_device(initial, site_kind):
    amount = initial.shape[0]
    along_x_part, along_y_part, along_z_part = speeds(lax.axis_index("vel") * amount, amount)
    distribution_table = initial
    kelvin_level = jnp.zeros(site_kind.shape, jnp.float32)
    signs = halo_signs(lax.axis_size("vel"), amount)
    for section in range(STEPS):
        if signs is None or distribution_table.shape[1] < 2:
            padded = with_halo(distribution_table, (("space", 1),), 2)
        else:
            padded = with_upwind_halo(distribution_table, signs)
        advected_distribution = transport(padded, along_x_part, along_y_part)
        distribution_table, kelvin_level = approach_increment(
            advected_distribution, site_kind, along_x_part, along_y_part, along_z_part
        )
    return (distribution_table, kelvin_level)


def solution(mesh):
    return jax.shard_map(
        per_device,
        mesh=mesh,
        in_specs=(P("vel", "space", None), P("space", None)),
        out_specs=(P("vel", "space", None), P("space", None)),
        check_vma=False,
    )
```

```python
import math

import jax
import numpy as np
import jax.numpy as jnp
from jax import lax
from jax.sharding import PartitionSpec as P


NVX = 24
STEPS = 2


speed_limit = 4.0
courant = 0.1
diffusivity_ratio = 2.0 / 3.0
power_law_index = 0.81
encounter_rate = 0.25
wall_kelvin = 1.0
inflow_concentration = 1.0
inflow_speed = 0.5
inflow_kelvin = 1.0


def with_halo(block, sides, width):
    for axis, dim in sides:
        count = lax.axis_size(axis)
        forward = [(i, i + 1) for i in range(count - 1)]
        backward = [(target, source) for source, target in forward]
        low = lax.ppermute(
            lax.slice_in_dim(block, block.shape[dim] - width, None, axis=dim), axis, forward
        )
        high = lax.ppermute(lax.slice_in_dim(block, 0, width, axis=dim), axis, backward)
        block = jnp.concatenate([low, block, high], axis=dim)
    return block


def halo_signs(vel_count, amount):
    spacing = 2.0 * speed_limit / (NVX - 1)
    signs = []
    for member in range(vel_count):
        index = np.arange(member * amount, (member + 1) * amount)
        along_x_part = np.float32(-speed_limit) + np.float32(spacing) * (index // (NVX * NVX)).astype(np.float32)
        if np.all(along_x_part > 0):
            signs.append(1)
        elif np.all(along_x_part < 0):
            signs.append(-1)
        else:
            return None
    return signs


def upwind_pieces(block, signs):
    count = lax.axis_size("space")
    rows = block.shape[1]
    forward = [(i, i + 1) for i in range(count - 1)]
    backward = [(target, source) for source, target in forward]
    low = lax.ppermute(block[:, rows - 1 :], "space", forward)
    high = lax.ppermute(block[:, :1], "space", backward)
    pairs = []
    for member, sign in enumerate(signs):
        for source, target in forward if sign > 0 else backward:
            pairs.append((member * count + source, member * count + target))
    positive = jnp.asarray(np.array(signs, np.int32))[lax.axis_index("vel")] > 0
    extra = lax.ppermute(
        jnp.where(positive, block[:, rows - 2 : rows - 1], block[:, 1:2]), ("vel", "space"), pairs
    )
    return extra, low, high


def with_upwind_halo(block, signs):
    extra, low, high = upwind_pieces(block, signs)
    return jnp.concatenate([extra, low, block, high, extra], axis=1)


def speeds(offset, amount):
    index = offset + jnp.arange(amount, dtype=jnp.int32)
    spacing = 2.0 * speed_limit / (NVX - 1)
    along_x_part = -speed_limit + spacing * (index // (NVX * NVX)).astype(jnp.float32)
    along_y_part = -speed_limit + spacing * (index // NVX % NVX).astype(jnp.float32)
    along_z_part = -speed_limit + spacing * (index % NVX).astype(jnp.float32)
    return (along_x_part, along_y_part, along_z_part)


def quad_weight():
    return (2.0 * speed_limit / (NVX - 1)) ** 3 / (2.0 * math.pi) ** 1.5


def minmod(left, right):
    return 0.5 * (jnp.sign(left) + jnp.sign(right)) * jnp.minimum(jnp.abs(left), jnp.abs(right))


def sweep(distribution_table, number, along):
    length = distribution_table.shape[along]

    def piece(source, low, high):
        return lax.slice_in_dim(source, low, high, axis=along)

    jumps = piece(distribution_table, 1, length) - piece(distribution_table, 0, length - 1)
    slopes = minmod(piece(jumps, 0, length - 2), piece(jumps, 1, length - 1))
    left_face = piece(distribution_table, 1, length - 2) + 0.5 * (1.0 - number) * piece(
        slopes, 0, length - 3
    )
    right_face = piece(distribution_table, 2, length - 1) - 0.5 * (1.0 + number) * piece(
        slopes, 1, length - 2
    )
    flux = number * jnp.where(number > 0, left_face, right_face)
    return piece(distribution_table, 2, length - 2) - (
        piece(flux, 1, length - 3) - piece(flux, 0, length - 4)
    )


def transport(padded, along_x_part, along_y_part):
    swept = sweep(padded, courant * along_x_part[:, None, None], 1)
    widened = jnp.pad(swept, ((0, 0), (0, 0), (2, 2)))
    return sweep(widened, courant * along_y_part[:, None, None], 2)


def xor_tree(values):
    while len(values) > 1:
        values = [values[2 * j] + values[2 * j + 1] for j in range(len(values) // 2)]
    return values[0]


def vel_sum(local):
    count = lax.axis_size("vel")
    if count & (count - 1):
        return lax.psum(local, "vel")
    bits = count.bit_length() - 1
    groups = []
    low = 0
    while low < bits:
        groups.append((low, min(2, bits - low)))
        low += 2
    for low, width in reversed(groups):
        values = [local]
        for member in range(1, 1 << width):
            mask = member << low
            values.append(lax.ppermute(local, "vel", [(i, i ^ mask) for i in range(count)]))
        local = xor_tree(values)
    return local


def moment_totals(advected_distribution, along_x_part, along_y_part, along_z_part):
    magnitude_squares = (
        along_x_part * along_x_part + along_y_part * along_y_part + along_z_part * along_z_part
    )
    ones = jnp.ones_like(along_x_part)
    table = quad_weight() * jnp.stack(
        [
            ones,
            along_x_part,
            along_y_part,
            along_z_part,
            magnitude_squares,
            along_x_part * along_x_part,
            along_y_part * along_y_part,
            along_z_part * along_z_part,
            along_x_part * along_y_part,
            along_x_part * along_z_part,
            along_y_part * along_z_part,
            along_x_part * magnitude_squares,
            along_y_part * magnitude_squares,
            along_z_part * magnitude_squares,
            jnp.zeros_like(along_x_part),
            jnp.zeros_like(along_x_part),
        ]
    )
    local = jnp.einsum("kv,vrc->krc", table, advected_distribution, precision=lax.Precision.HIGHEST)
    return vel_sum(local)


def derived_moments(totals):
    particle_concentration = totals[0]
    average_drift_x = totals[1] / particle_concentration
    average_drift_y = totals[2] / particle_concentration
    average_drift_z = totals[3] / particle_concentration
    energy = totals[4]
    drift_square = (
        average_drift_x * average_drift_x
        + average_drift_y * average_drift_y
        + average_drift_z * average_drift_z
    )
    kelvin_level = (energy / particle_concentration - drift_square) / 3.0
    xx, yy, zz, xy, xz, yz = (totals[k] for k in range(5, 11))
    drift = (average_drift_x, average_drift_y, average_drift_z)
    second = ((xx, xy, xz), (xy, yy, yz), (xz, yz, zz))
    common = 2.0 * particle_concentration * drift_square
    conductive_transfer = jnp.stack(
        [
            0.5
            * (
                totals[11 + i]
                - 2.0 * (drift[0] * second[i][0] + drift[1] * second[i][1] + drift[2] * second[i][2])
                - drift[i] * energy
                + drift[i] * common
            )
            for i in range(3)
        ]
    )
    return (
        particle_concentration,
        average_drift_x,
        average_drift_y,
        average_drift_z,
        kelvin_level,
        conductive_transfer,
    )


def approach_increment(
    advected_distribution, kind_labels, along_x_part, along_y_part, along_z_part, totals
):
    (
        particle_concentration,
        average_drift_x,
        average_drift_y,
        average_drift_z,
        kelvin_level,
        conductive_transfer,
    ) = derived_moments(totals)
    rel_x = along_x_part[:, None, None] - average_drift_x[None]
    rel_y = along_y_part[:, None, None] - average_drift_y[None]
    rel_z = along_z_part[:, None, None] - average_drift_z[None]
    relative_magnitude_square = rel_x * rel_x + rel_y * rel_y + rel_z * rel_z
    stress_scalar_grid = particle_concentration * kelvin_level
    gaussian_local_balance = (
        particle_concentration
        * kelvin_level ** (-1.5)
        * jnp.exp(-relative_magnitude_square / (2.0 * kelvin_level))
    )
    conductive_vector_slot = (
        rel_x * conductive_transfer[0]
        + rel_y * conductive_transfer[1]
        + rel_z * conductive_transfer[2]
    )
    corrected_goal_distribution = gaussian_local_balance * (
        1.0
        + (1.0 - diffusivity_ratio)
        * conductive_vector_slot
        * (relative_magnitude_square / kelvin_level - 5.0)
        / (5.0 * stress_scalar_grid * kelvin_level)
    )
    approach_rate = (
        encounter_rate * particle_concentration * kelvin_level ** (1.0 - power_law_index)
    )
    relaxed = advected_distribution + approach_rate * (
        corrected_goal_distribution - advected_distribution
    )
    magnitude_squares = (
        along_x_part * along_x_part + along_y_part * along_y_part + along_z_part * along_z_part
    )[:, None, None]
    wall_distribution = (
        particle_concentration
        * wall_kelvin ** (-1.5)
        * jnp.exp(-magnitude_squares / (2.0 * wall_kelvin))
    )
    inflow_magnitude_square = (
        (along_x_part - inflow_speed) ** 2
        + along_y_part * along_y_part
        + along_z_part * along_z_part
    )[:, None, None]
    inflow_distribution = (
        inflow_concentration
        * inflow_kelvin ** (-1.5)
        * jnp.exp(-inflow_magnitude_square / (2.0 * inflow_kelvin))
    )
    revised_distribution = jnp.where(
        kind_labels == 1,
        wall_distribution,
        jnp.where(kind_labels == 2, inflow_distribution, relaxed),
    )
    return (revised_distribution, kelvin_level)


def per_device(initial, site_kind):
    amount = initial.shape[0]
    along_x_part, along_y_part, along_z_part = speeds(lax.axis_index("vel") * amount, amount)
    distribution_table = initial
    kelvin_level = jnp.zeros(site_kind.shape, jnp.float32)
    rows = distribution_table.shape[1]
    signs = halo_signs(lax.axis_size("vel"), amount)
    if signs is None or rows < 2:
        for _ in range(STEPS):
            padded = with_halo(distribution_table, (("space", 1),), 2)
            advected_distribution = transport(padded, along_x_part, along_y_part)
            totals = moment_totals(advected_distribution, along_x_part, along_y_part, along_z_part)
            distribution_table, kelvin_level = approach_increment(
                advected_distribution, site_kind, along_x_part, along_y_part, along_z_part, totals
            )
        return (distribution_table, kelvin_level)
    count = lax.axis_size("space")
    positive = jnp.asarray(np.array(signs, np.int32))[lax.axis_index("vel")] > 0
    place = lax.axis_index("space") * rows + jnp.array([-2, -1, rows, rows + 1])
    keep = (place >= 0) & (place < count * rows)
    keep = keep & jnp.where(positive, jnp.arange(4) != 3, jnp.arange(4) != 0)
    carried = jnp.concatenate([initial, site_kind.astype(jnp.float32)[None]], axis=0)
    padded_all = with_upwind_halo(carried, signs)
    padded = padded_all[:amount]
    kinds_all = padded_all[amount]
    halo_kinds = jnp.concatenate([kinds_all[:2], kinds_all[rows + 2 :]], axis=0).astype(jnp.int32)
    for section in range(STEPS):
        advected_distribution = transport(padded, along_x_part, along_y_part)
        if section + 1 < STEPS:
            extra, low, high = upwind_pieces(advected_distribution, signs)
        totals = moment_totals(advected_distribution, along_x_part, along_y_part, along_z_part)
        if section + 1 < STEPS:
            total_extra, total_low, total_high = upwind_pieces(totals, signs)
            own, _ = approach_increment(
                advected_distribution, site_kind, along_x_part, along_y_part, along_z_part, totals
            )
            halo, _ = approach_increment(
                jnp.concatenate([extra, low, high, extra], axis=1),
                halo_kinds,
                along_x_part,
                along_y_part,
                along_z_part,
                jnp.concatenate([total_extra, total_low, total_high, total_extra], axis=1),
            )
            halo = jnp.where(keep[None, :, None], halo, 0.0)
            padded = jnp.concatenate([halo[:, :2], own, halo[:, 2:]], axis=1)
        else:
            distribution_table, kelvin_level = approach_increment(
                advected_distribution, site_kind, along_x_part, along_y_part, along_z_part, totals
            )
    return (distribution_table, kelvin_level)


def solution(mesh):
    return jax.shard_map(
        per_device,
        mesh=mesh,
        in_specs=(P("vel", "space", None), P("space", None)),
        out_specs=(P("vel", "space", None), P("space", None)),
        check_vma=False,
    )
```

```python
import math

import jax
import numpy as np
import jax.numpy as jnp
from jax import lax
from jax.sharding import PartitionSpec as P

NVX = 24
STEPS = 2


speed_limit = 4.0
courant = 0.1
diffusivity_ratio = 2.0 / 3.0
power_law_index = 0.81
encounter_rate = 0.25
wall_kelvin = 1.0
inflow_concentration = 1.0
inflow_speed = 0.5
inflow_kelvin = 1.0


def with_halo(block, sides, width):
    for axis, dim in sides:
        count = lax.axis_size(axis)
        forward = [(i, i + 1) for i in range(count - 1)]
        backward = [(target, source) for source, target in forward]
        low = lax.ppermute(
            lax.slice_in_dim(block, block.shape[dim] - width, None, axis=dim), axis, forward
        )
        high = lax.ppermute(lax.slice_in_dim(block, 0, width, axis=dim), axis, backward)
        block = jnp.concatenate([low, block, high], axis=dim)
    return block


def halo_signs(vel_count, amount):
    spacing = 2.0 * speed_limit / (NVX - 1)
    signs = []
    for member in range(vel_count):
        index = np.arange(member * amount, (member + 1) * amount)
        along_x_part = np.float32(-speed_limit) + np.float32(spacing) * (index // (NVX * NVX)).astype(np.float32)
        if np.all(along_x_part > 0):
            signs.append(1)
        elif np.all(along_x_part < 0):
            signs.append(-1)
        else:
            return None
    return signs


def with_upwind_halo(block, signs):
    count = lax.axis_size("space")
    rows = block.shape[1]
    forward = [(i, i + 1) for i in range(count - 1)]
    backward = [(target, source) for source, target in forward]
    low = lax.ppermute(block[:, rows - 1 :], "space", forward)
    high = lax.ppermute(block[:, :1], "space", backward)
    pairs = []
    for member, sign in enumerate(signs):
        for source, target in forward if sign > 0 else backward:
            pairs.append((member * count + source, member * count + target))
    positive = jnp.asarray(np.array(signs, np.int32))[lax.axis_index("vel")] > 0
    extra = lax.ppermute(
        jnp.where(positive, block[:, rows - 2 : rows - 1], block[:, 1:2]), ("vel", "space"), pairs
    )
    return jnp.concatenate([extra, low, block, high, extra], axis=1)


def speeds(offset, amount):
    index = offset + jnp.arange(amount, dtype=jnp.int32)
    spacing = 2.0 * speed_limit / (NVX - 1)
    along_x_part = -speed_limit + spacing * (index // (NVX * NVX)).astype(jnp.float32)
    along_y_part = -speed_limit + spacing * (index // NVX % NVX).astype(jnp.float32)
    along_z_part = -speed_limit + spacing * (index % NVX).astype(jnp.float32)
    return (along_x_part, along_y_part, along_z_part)


def quad_weight():
    return (2.0 * speed_limit / (NVX - 1)) ** 3 / (2.0 * math.pi) ** 1.5


def minmod(left, right):
    return jnp.maximum(jnp.minimum(left, right), jnp.minimum(jnp.maximum(left, right), 0.0))


def sweep(distribution_table, number, along):
    length = distribution_table.shape[along]

    def piece(source, low, high):
        return lax.slice_in_dim(source, low, high, axis=along)

    jumps = piece(distribution_table, 1, length) - piece(distribution_table, 0, length - 1)
    slopes = minmod(piece(jumps, 0, length - 2), piece(jumps, 1, length - 1))
    left_face = piece(distribution_table, 1, length - 2) + 0.5 * (1.0 - number) * piece(
        slopes, 0, length - 3
    )
    right_face = piece(distribution_table, 2, length - 1) - 0.5 * (1.0 + number) * piece(
        slopes, 1, length - 2
    )
    flux = number * jnp.where(number > 0, left_face, right_face)
    return piece(distribution_table, 2, length - 2) - (
        piece(flux, 1, length - 3) - piece(flux, 0, length - 4)
    )


def transport(padded, along_x_part, along_y_part):
    swept = sweep(padded, courant * along_x_part[:, None, None], 1)
    widened = jnp.pad(swept, ((0, 0), (0, 0), (2, 2)))
    return sweep(widened, courant * along_y_part[:, None, None], 2)


def xor_tree(values):
    while len(values) > 1:
        values = [values[2 * j] + values[2 * j + 1] for j in range(len(values) // 2)]
    return values[0]


def vel_sum(local):
    count = lax.axis_size("vel")
    if count & (count - 1):
        return lax.psum(local, "vel")
    bits = count.bit_length() - 1
    groups = []
    low = 0
    while low < bits:
        groups.append((low, min(2, bits - low)))
        low += 2
    for low, width in reversed(groups):
        values = [local]
        for member in range(1, 1 << width):
            mask = member << low
            values.append(lax.ppermute(local, "vel", [(i, i ^ mask) for i in range(count)]))
        local = xor_tree(values)
    return local


def macroscopic_moments(advected_distribution, along_x_part, along_y_part, along_z_part):
    magnitude_squares = (
        along_x_part * along_x_part + along_y_part * along_y_part + along_z_part * along_z_part
    )
    ones = jnp.ones_like(along_x_part)
    table = quad_weight() * jnp.stack(
        [
            ones,
            along_x_part,
            along_y_part,
            along_z_part,
            magnitude_squares,
            along_x_part * along_x_part,
            along_y_part * along_y_part,
            along_z_part * along_z_part,
            along_x_part * along_y_part,
            along_x_part * along_z_part,
            along_y_part * along_z_part,
            along_x_part * magnitude_squares,
            along_y_part * magnitude_squares,
            along_z_part * magnitude_squares,
            jnp.zeros_like(along_x_part),
            jnp.zeros_like(along_x_part),
        ]
    )
    local = jnp.einsum("kv,vrc->krc", table, advected_distribution, precision=lax.Precision.HIGHEST)
    totals = vel_sum(local)
    particle_concentration = totals[0]
    average_drift_x = totals[1] / particle_concentration
    average_drift_y = totals[2] / particle_concentration
    average_drift_z = totals[3] / particle_concentration
    energy = totals[4]
    drift_square = (
        average_drift_x * average_drift_x
        + average_drift_y * average_drift_y
        + average_drift_z * average_drift_z
    )
    kelvin_level = (energy / particle_concentration - drift_square) / 3.0
    xx, yy, zz, xy, xz, yz = (totals[k] for k in range(5, 11))
    drift = (average_drift_x, average_drift_y, average_drift_z)
    second = ((xx, xy, xz), (xy, yy, yz), (xz, yz, zz))
    common = 2.0 * particle_concentration * drift_square
    conductive_transfer = jnp.stack(
        [
            0.5
            * (
                totals[11 + i]
                - 2.0 * (drift[0] * second[i][0] + drift[1] * second[i][1] + drift[2] * second[i][2])
                - drift[i] * energy
                + drift[i] * common
            )
            for i in range(3)
        ]
    )
    return (
        particle_concentration,
        average_drift_x,
        average_drift_y,
        average_drift_z,
        kelvin_level,
        conductive_transfer,
    )


def approach_increment(
    advected_distribution, kind_labels, along_x_part, along_y_part, along_z_part
):
    (
        particle_concentration,
        average_drift_x,
        average_drift_y,
        average_drift_z,
        kelvin_level,
        conductive_transfer,
    ) = macroscopic_moments(advected_distribution, along_x_part, along_y_part, along_z_part)
    rel_x = along_x_part[:, None, None] - average_drift_x[None]
    rel_y = along_y_part[:, None, None] - average_drift_y[None]
    rel_z = along_z_part[:, None, None] - average_drift_z[None]
    relative_magnitude_square = rel_x * rel_x + rel_y * rel_y + rel_z * rel_z
    stress_scalar_grid = particle_concentration * kelvin_level
    gaussian_local_balance = (
        particle_concentration
        * kelvin_level ** (-1.5)
        * jnp.exp(-relative_magnitude_square / (2.0 * kelvin_level))
    )
    conductive_vector_slot = (
        rel_x * conductive_transfer[0]
        + rel_y * conductive_transfer[1]
        + rel_z * conductive_transfer[2]
    )
    corrected_goal_distribution = gaussian_local_balance * (
        1.0
        + (1.0 - diffusivity_ratio)
        * conductive_vector_slot
        * (relative_magnitude_square / kelvin_level - 5.0)
        / (5.0 * stress_scalar_grid * kelvin_level)
    )
    approach_rate = (
        encounter_rate * particle_concentration * kelvin_level ** (1.0 - power_law_index)
    )
    relaxed = advected_distribution + approach_rate * (
        corrected_goal_distribution - advected_distribution
    )
    magnitude_squares = (
        along_x_part * along_x_part + along_y_part * along_y_part + along_z_part * along_z_part
    )[:, None, None]
    wall_distribution = (
        particle_concentration
        * wall_kelvin ** (-1.5)
        * jnp.exp(-magnitude_squares / (2.0 * wall_kelvin))
    )
    inflow_magnitude_square = (
        (along_x_part - inflow_speed) ** 2
        + along_y_part * along_y_part
        + along_z_part * along_z_part
    )[:, None, None]
    inflow_distribution = (
        inflow_concentration
        * inflow_kelvin ** (-1.5)
        * jnp.exp(-inflow_magnitude_square / (2.0 * inflow_kelvin))
    )
    revised_distribution = jnp.where(
        kind_labels == 1,
        wall_distribution,
        jnp.where(kind_labels == 2, inflow_distribution, relaxed),
    )
    return (revised_distribution, kelvin_level)


def per_device(initial, site_kind):
    amount = initial.shape[0]
    along_x_part, along_y_part, along_z_part = speeds(lax.axis_index("vel") * amount, amount)
    distribution_table = initial
    kelvin_level = jnp.zeros(site_kind.shape, jnp.float32)
    signs = halo_signs(lax.axis_size("vel"), amount)
    for section in range(STEPS):
        if signs is None or distribution_table.shape[1] < 2:
            padded = with_halo(distribution_table, (("space", 1),), 2)
        else:
            padded = with_upwind_halo(distribution_table, signs)
        advected_distribution = transport(padded, along_x_part, along_y_part)
        distribution_table, kelvin_level = approach_increment(
            advected_distribution, site_kind, along_x_part, along_y_part, along_z_part
        )
    return (distribution_table, kelvin_level)


def solution(mesh):
    return jax.shard_map(
        per_device,
        mesh=mesh,
        in_specs=(P("vel", "space", None), P("space", None)),
        out_specs=(P("vel", "space", None), P("space", None)),
        check_vma=False,
    )
```

```python
import math
import os

import jax
import numpy as np
import jax.numpy as jnp
from jax import lax
from jax.experimental import pallas as pl
from jax.experimental.pallas import tpu as pltpu
from jax.sharding import PartitionSpec as P

NVX = 24
STEPS = 2


speed_limit = 4.0
courant = 0.1
diffusivity_ratio = 2.0 / 3.0
power_law_index = 0.81
encounter_rate = 0.25
wall_kelvin = 1.0
inflow_concentration = 1.0
inflow_speed = 0.5
inflow_kelvin = 1.0


def with_halo(block, sides, width):
    for axis, dim in sides:
        count = lax.axis_size(axis)
        forward = [(i, i + 1) for i in range(count - 1)]
        backward = [(target, source) for source, target in forward]
        low = lax.ppermute(
            lax.slice_in_dim(block, block.shape[dim] - width, None, axis=dim), axis, forward
        )
        high = lax.ppermute(lax.slice_in_dim(block, 0, width, axis=dim), axis, backward)
        block = jnp.concatenate([low, block, high], axis=dim)
    return block


def halo_signs(vel_count, amount):
    spacing = 2.0 * speed_limit / (NVX - 1)
    signs = []
    for member in range(vel_count):
        index = np.arange(member * amount, (member + 1) * amount)
        along_x_part = np.float32(-speed_limit) + np.float32(spacing) * (index // (NVX * NVX)).astype(np.float32)
        if np.all(along_x_part > 0):
            signs.append(1)
        elif np.all(along_x_part < 0):
            signs.append(-1)
        else:
            return None
    return signs


def with_upwind_halo(block, signs):
    count = lax.axis_size("space")
    rows = block.shape[1]
    forward = [(i, i + 1) for i in range(count - 1)]
    backward = [(target, source) for source, target in forward]
    low = lax.ppermute(block[:, rows - 1 :], "space", forward)
    high = lax.ppermute(block[:, :1], "space", backward)
    pairs = []
    for member, sign in enumerate(signs):
        for source, target in forward if sign > 0 else backward:
            pairs.append((member * count + source, member * count + target))
    positive = jnp.asarray(np.array(signs, np.int32))[lax.axis_index("vel")] > 0
    extra = lax.ppermute(
        jnp.where(positive, block[:, rows - 2 : rows - 1], block[:, 1:2]), ("vel", "space"), pairs
    )
    return jnp.concatenate([extra, low, block, high, extra], axis=1)


def speeds(offset, amount):
    index = offset + jnp.arange(amount, dtype=jnp.int32)
    spacing = 2.0 * speed_limit / (NVX - 1)
    along_x_part = -speed_limit + spacing * (index // (NVX * NVX)).astype(jnp.float32)
    along_y_part = -speed_limit + spacing * (index // NVX % NVX).astype(jnp.float32)
    along_z_part = -speed_limit + spacing * (index % NVX).astype(jnp.float32)
    return (along_x_part, along_y_part, along_z_part)


def quad_weight():
    return (2.0 * speed_limit / (NVX - 1)) ** 3 / (2.0 * math.pi) ** 1.5


def minmod(left, right):
    return jnp.maximum(jnp.minimum(left, right), jnp.minimum(jnp.maximum(left, right), 0.0))


def sweep(distribution_table, number, along):
    length = distribution_table.shape[along]

    def piece(source, low, high):
        return lax.slice_in_dim(source, low, high, axis=along)

    jumps = piece(distribution_table, 1, length) - piece(distribution_table, 0, length - 1)
    slopes = minmod(piece(jumps, 0, length - 2), piece(jumps, 1, length - 1))
    left_face = piece(distribution_table, 1, length - 2) + 0.5 * (1.0 - number) * piece(
        slopes, 0, length - 3
    )
    right_face = piece(distribution_table, 2, length - 1) - 0.5 * (1.0 + number) * piece(
        slopes, 1, length - 2
    )
    flux = number * jnp.where(number > 0, left_face, right_face)
    return piece(distribution_table, 2, length - 2) - (
        piece(flux, 1, length - 3) - piece(flux, 0, length - 4)
    )


def face_flux(number, lower, upper, lower_slope, upper_slope):
    return number * jnp.where(
        number > 0,
        lower + 0.5 * (1.0 - number) * lower_slope,
        upper - 0.5 * (1.0 + number) * upper_slope,
    )


def lane_sweep_kernel(number_ref, swept_ref, out_ref):
    rows, block, width = swept_ref.shape
    lane = lax.broadcasted_iota(jnp.int32, (8, width), 1)
    first = lane == 0
    last = lane == width - 1

    def slab(i, carry):
        part = pl.ds(pl.multiple_of(i * 8, 8), 8)
        number = jnp.broadcast_to(number_ref[part, :], (8, width))
        for k in range(rows):
            values = swept_ref[k, part, :]
            before = jnp.where(first, 0.0, pltpu.roll(values, 1, 1))
            after = jnp.where(last, 0.0, pltpu.roll(values, width - 1, 1))
            slope = minmod(values - before, after - values)
            slope_before = jnp.where(first, 0.0, pltpu.roll(slope, 1, 1))
            slope_after = jnp.where(last, 0.0, pltpu.roll(slope, width - 1, 1))
            flux_after = face_flux(number, values, after, slope, slope_after)
            flux_before = face_flux(number, before, values, slope_before, slope)
            out_ref[k, part, :] = values - (flux_after - flux_before)
        return carry

    lax.fori_loop(0, block // 8, slab, 0)


def transport(padded, along_x_part, along_y_part):
    swept = sweep(padded, courant * along_x_part[:, None, None], 1)
    amount, rows, width = swept.shape
    if amount % 8 or width % 128:
        widened = jnp.pad(swept, ((0, 0), (0, 0), (2, 2)))
        return sweep(widened, courant * along_y_part[:, None, None], 2)
    block = 96 if amount % 96 == 0 else 8
    stacked = jnp.transpose(swept, (1, 0, 2))
    shifted = pl.pallas_call(
        lane_sweep_kernel,
        grid=(amount // block,),
        in_specs=[
            pl.BlockSpec((block, 1), lambda i: (i, 0)),
            pl.BlockSpec((rows, block, width), lambda i: (0, i, 0)),
        ],
        out_specs=pl.BlockSpec((rows, block, width), lambda i: (0, i, 0)),
        out_shape=jax.ShapeDtypeStruct((rows, amount, width), swept.dtype),
        interpret=os.environ.get("SOLUTION_INTERPRET") == "1",
    )((courant * along_y_part)[:, None], stacked)
    return jnp.transpose(shifted, (1, 0, 2))


def xor_tree(values):
    while len(values) > 1:
        values = [values[2 * j] + values[2 * j + 1] for j in range(len(values) // 2)]
    return values[0]


def vel_sum(local):
    count = lax.axis_size("vel")
    if count & (count - 1):
        return lax.psum(local, "vel")
    bits = count.bit_length() - 1
    groups = []
    low = 0
    while low < bits:
        groups.append((low, min(2, bits - low)))
        low += 2
    for low, width in reversed(groups):
        values = [local]
        for member in range(1, 1 << width):
            mask = member << low
            values.append(lax.ppermute(local, "vel", [(i, i ^ mask) for i in range(count)]))
        local = xor_tree(values)
    return local


def macroscopic_moments(advected_distribution, along_x_part, along_y_part, along_z_part):
    magnitude_squares = (
        along_x_part * along_x_part + along_y_part * along_y_part + along_z_part * along_z_part
    )
    ones = jnp.ones_like(along_x_part)
    table = quad_weight() * jnp.stack(
        [
            ones,
            along_x_part,
            along_y_part,
            along_z_part,
            magnitude_squares,
            along_x_part * along_x_part,
            along_y_part * along_y_part,
            along_z_part * along_z_part,
            along_x_part * along_y_part,
            along_x_part * along_z_part,
            along_y_part * along_z_part,
            along_x_part * magnitude_squares,
            along_y_part * magnitude_squares,
            along_z_part * magnitude_squares,
            jnp.zeros_like(along_x_part),
            jnp.zeros_like(along_x_part),
        ]
    )
    local = jnp.einsum("kv,vrc->krc", table, advected_distribution, precision=lax.Precision.HIGHEST)
    totals = vel_sum(local)
    particle_concentration = totals[0]
    average_drift_x = totals[1] / particle_concentration
    average_drift_y = totals[2] / particle_concentration
    average_drift_z = totals[3] / particle_concentration
    energy = totals[4]
    drift_square = (
        average_drift_x * average_drift_x
        + average_drift_y * average_drift_y
        + average_drift_z * average_drift_z
    )
    kelvin_level = (energy / particle_concentration - drift_square) / 3.0
    xx, yy, zz, xy, xz, yz = (totals[k] for k in range(5, 11))
    drift = (average_drift_x, average_drift_y, average_drift_z)
    second = ((xx, xy, xz), (xy, yy, yz), (xz, yz, zz))
    common = 2.0 * particle_concentration * drift_square
    conductive_transfer = jnp.stack(
        [
            0.5
            * (
                totals[11 + i]
                - 2.0 * (drift[0] * second[i][0] + drift[1] * second[i][1] + drift[2] * second[i][2])
                - drift[i] * energy
                + drift[i] * common
            )
            for i in range(3)
        ]
    )
    return (
        particle_concentration,
        average_drift_x,
        average_drift_y,
        average_drift_z,
        kelvin_level,
        conductive_transfer,
    )


def approach_increment(
    advected_distribution, kind_labels, along_x_part, along_y_part, along_z_part
):
    (
        particle_concentration,
        average_drift_x,
        average_drift_y,
        average_drift_z,
        kelvin_level,
        conductive_transfer,
    ) = macroscopic_moments(advected_distribution, along_x_part, along_y_part, along_z_part)
    rel_x = along_x_part[:, None, None] - average_drift_x[None]
    rel_y = along_y_part[:, None, None] - average_drift_y[None]
    rel_z = along_z_part[:, None, None] - average_drift_z[None]
    relative_magnitude_square = rel_x * rel_x + rel_y * rel_y + rel_z * rel_z
    stress_scalar_grid = particle_concentration * kelvin_level
    gaussian_local_balance = (
        particle_concentration
        * kelvin_level ** (-1.5)
        * jnp.exp(-relative_magnitude_square / (2.0 * kelvin_level))
    )
    conductive_vector_slot = (
        rel_x * conductive_transfer[0]
        + rel_y * conductive_transfer[1]
        + rel_z * conductive_transfer[2]
    )
    corrected_goal_distribution = gaussian_local_balance * (
        1.0
        + (1.0 - diffusivity_ratio)
        * conductive_vector_slot
        * (relative_magnitude_square / kelvin_level - 5.0)
        / (5.0 * stress_scalar_grid * kelvin_level)
    )
    approach_rate = (
        encounter_rate * particle_concentration * kelvin_level ** (1.0 - power_law_index)
    )
    relaxed = advected_distribution + approach_rate * (
        corrected_goal_distribution - advected_distribution
    )
    magnitude_squares = (
        along_x_part * along_x_part + along_y_part * along_y_part + along_z_part * along_z_part
    )[:, None, None]
    wall_distribution = (
        particle_concentration
        * wall_kelvin ** (-1.5)
        * jnp.exp(-magnitude_squares / (2.0 * wall_kelvin))
    )
    inflow_magnitude_square = (
        (along_x_part - inflow_speed) ** 2
        + along_y_part * along_y_part
        + along_z_part * along_z_part
    )[:, None, None]
    inflow_distribution = (
        inflow_concentration
        * inflow_kelvin ** (-1.5)
        * jnp.exp(-inflow_magnitude_square / (2.0 * inflow_kelvin))
    )
    revised_distribution = jnp.where(
        kind_labels == 1,
        wall_distribution,
        jnp.where(kind_labels == 2, inflow_distribution, relaxed),
    )
    return (revised_distribution, kelvin_level)


def per_device(initial, site_kind):
    amount = initial.shape[0]
    along_x_part, along_y_part, along_z_part = speeds(lax.axis_index("vel") * amount, amount)
    distribution_table = initial
    kelvin_level = jnp.zeros(site_kind.shape, jnp.float32)
    signs = halo_signs(lax.axis_size("vel"), amount)
    for section in range(STEPS):
        if signs is None or distribution_table.shape[1] < 2:
            padded = with_halo(distribution_table, (("space", 1),), 2)
        else:
            padded = with_upwind_halo(distribution_table, signs)
        advected_distribution = transport(padded, along_x_part, along_y_part)
        distribution_table, kelvin_level = approach_increment(
            advected_distribution, site_kind, along_x_part, along_y_part, along_z_part
        )
    return (distribution_table, kelvin_level)


def solution(mesh):
    return jax.shard_map(
        per_device,
        mesh=mesh,
        in_specs=(P("vel", "space", None), P("space", None)),
        out_specs=(P("vel", "space", None), P("space", None)),
        check_vma=False,
    )
```

```python
import math

import jax
import numpy as np
import jax.numpy as jnp
from jax import lax
from jax.sharding import PartitionSpec as P

NVX = 24
STEPS = 2


speed_limit = 4.0
courant = 0.1
diffusivity_ratio = 2.0 / 3.0
power_law_index = 0.81
encounter_rate = 0.25
wall_kelvin = 1.0
inflow_concentration = 1.0
inflow_speed = 0.5
inflow_kelvin = 1.0


def with_halo(block, sides, width):
    for axis, dim in sides:
        count = lax.axis_size(axis)
        forward = [(i, i + 1) for i in range(count - 1)]
        backward = [(target, source) for source, target in forward]
        low = lax.ppermute(
            lax.slice_in_dim(block, block.shape[dim] - width, None, axis=dim), axis, forward
        )
        high = lax.ppermute(lax.slice_in_dim(block, 0, width, axis=dim), axis, backward)
        block = jnp.concatenate([low, block, high], axis=dim)
    return block


def halo_signs(vel_count, amount):
    spacing = 2.0 * speed_limit / (NVX - 1)
    signs = []
    for member in range(vel_count):
        index = np.arange(member * amount, (member + 1) * amount)
        along_x_part = np.float32(-speed_limit) + np.float32(spacing) * (index // (NVX * NVX)).astype(np.float32)
        if np.all(along_x_part > 0):
            signs.append(1)
        elif np.all(along_x_part < 0):
            signs.append(-1)
        else:
            return None
    return signs


def with_upwind_halo(block, signs):
    count = lax.axis_size("space")
    rows = block.shape[1]
    forward = [(i, i + 1) for i in range(count - 1)]
    backward = [(target, source) for source, target in forward]
    low = lax.ppermute(block[:, rows - 1 :], "space", forward)
    high = lax.ppermute(block[:, :1], "space", backward)
    pairs = []
    for member, sign in enumerate(signs):
        for source, target in forward if sign > 0 else backward:
            pairs.append((member * count + source, member * count + target))
    positive = jnp.asarray(np.array(signs, np.int32))[lax.axis_index("vel")] > 0
    extra = lax.ppermute(
        jnp.where(positive, block[:, rows - 2 : rows - 1], block[:, 1:2]), ("vel", "space"), pairs
    )
    return jnp.concatenate([extra, low, block, high, extra], axis=1)


def speeds(offset, amount):
    index = offset + jnp.arange(amount, dtype=jnp.int32)
    spacing = 2.0 * speed_limit / (NVX - 1)
    along_x_part = -speed_limit + spacing * (index // (NVX * NVX)).astype(jnp.float32)
    along_y_part = -speed_limit + spacing * (index // NVX % NVX).astype(jnp.float32)
    along_z_part = -speed_limit + spacing * (index % NVX).astype(jnp.float32)
    return (along_x_part, along_y_part, along_z_part)


def quad_weight():
    return (2.0 * speed_limit / (NVX - 1)) ** 3 / (2.0 * math.pi) ** 1.5


def minmod(left, right):
    return jnp.maximum(jnp.minimum(left, right), jnp.minimum(jnp.maximum(left, right), 0.0))


def sweep(distribution_table, number, along):
    length = distribution_table.shape[along]

    def piece(source, low, high):
        return lax.slice_in_dim(source, low, high, axis=along)

    jumps = piece(distribution_table, 1, length) - piece(distribution_table, 0, length - 1)
    slopes = minmod(piece(jumps, 0, length - 2), piece(jumps, 1, length - 1))
    left_face = piece(distribution_table, 1, length - 2) + 0.5 * (1.0 - number) * piece(
        slopes, 0, length - 3
    )
    right_face = piece(distribution_table, 2, length - 1) - 0.5 * (1.0 + number) * piece(
        slopes, 1, length - 2
    )
    flux = number * jnp.where(number > 0, left_face, right_face)
    return piece(distribution_table, 2, length - 2) - (
        piece(flux, 1, length - 3) - piece(flux, 0, length - 4)
    )


def transport(padded, along_x_part, along_y_part):
    swept = sweep(padded, courant * along_x_part[:, None, None], 1)
    widened = jnp.pad(swept, ((0, 0), (0, 0), (2, 2)))
    return sweep(widened, courant * along_y_part[:, None, None], 2)


def xor_tree(values):
    while len(values) > 1:
        values = [values[2 * j] + values[2 * j + 1] for j in range(len(values) // 2)]
    return values[0]


def vel_sum(local):
    count = lax.axis_size("vel")
    if count & (count - 1):
        return lax.psum(local, "vel")
    bits = count.bit_length() - 1
    groups = []
    low = 0
    while low < bits:
        groups.append((low, min(2, bits - low)))
        low += 2
    for low, width in reversed(groups):
        values = [local]
        for member in range(1, 1 << width):
            mask = member << low
            values.append(lax.ppermute(local, "vel", [(i, i ^ mask) for i in range(count)]))
        local = xor_tree(values)
    return local


def macroscopic_moments(advected_distribution, along_x_part, along_y_part, along_z_part):
    magnitude_squares = (
        along_x_part * along_x_part + along_y_part * along_y_part + along_z_part * along_z_part
    )
    ones = jnp.ones_like(along_x_part)
    table = quad_weight() * jnp.stack(
        [
            ones,
            along_x_part,
            along_y_part,
            along_z_part,
            magnitude_squares,
            along_x_part * along_x_part,
            along_y_part * along_y_part,
            along_z_part * along_z_part,
            along_x_part * along_y_part,
            along_x_part * along_z_part,
            along_y_part * along_z_part,
            along_x_part * magnitude_squares,
            along_y_part * magnitude_squares,
            along_z_part * magnitude_squares,
            jnp.zeros_like(along_x_part),
            jnp.zeros_like(along_x_part),
        ]
    )
    local = jnp.einsum("kv,vrc->krc", table, advected_distribution, precision=lax.Precision.HIGHEST)
    totals = vel_sum(local)
    particle_concentration = totals[0]
    average_drift_x = totals[1] / particle_concentration
    average_drift_y = totals[2] / particle_concentration
    average_drift_z = totals[3] / particle_concentration
    energy = totals[4]
    drift_square = (
        average_drift_x * average_drift_x
        + average_drift_y * average_drift_y
        + average_drift_z * average_drift_z
    )
    kelvin_level = (energy / particle_concentration - drift_square) / 3.0
    xx, yy, zz, xy, xz, yz = (totals[k] for k in range(5, 11))
    drift = (average_drift_x, average_drift_y, average_drift_z)
    second = ((xx, xy, xz), (xy, yy, yz), (xz, yz, zz))
    common = 2.0 * particle_concentration * drift_square
    conductive_transfer = jnp.stack(
        [
            0.5
            * (
                totals[11 + i]
                - 2.0 * (drift[0] * second[i][0] + drift[1] * second[i][1] + drift[2] * second[i][2])
                - drift[i] * energy
                + drift[i] * common
            )
            for i in range(3)
        ]
    )
    return (
        particle_concentration,
        average_drift_x,
        average_drift_y,
        average_drift_z,
        kelvin_level,
        conductive_transfer,
    )


def approach_increment(
    advected_distribution, kind_labels, along_x_part, along_y_part, along_z_part
):
    (
        particle_concentration,
        average_drift_x,
        average_drift_y,
        average_drift_z,
        kelvin_level,
        conductive_transfer,
    ) = macroscopic_moments(advected_distribution, along_x_part, along_y_part, along_z_part)
    rel_x = along_x_part[:, None, None] - average_drift_x[None]
    rel_y = along_y_part[:, None, None] - average_drift_y[None]
    rel_z = along_z_part[:, None, None] - average_drift_z[None]
    relative_magnitude_square = rel_x * rel_x + rel_y * rel_y + rel_z * rel_z
    stress_scalar_grid = particle_concentration * kelvin_level
    inverse_level = 1.0 / kelvin_level
    half_inverse_level = 1.0 / (2.0 * kelvin_level)
    inverse_scale = 1.0 / (5.0 * stress_scalar_grid * kelvin_level)
    gaussian_local_balance = (
        particle_concentration
        * kelvin_level ** (-1.5)
        * jnp.exp(-relative_magnitude_square * half_inverse_level)
    )
    conductive_vector_slot = (
        rel_x * conductive_transfer[0]
        + rel_y * conductive_transfer[1]
        + rel_z * conductive_transfer[2]
    )
    corrected_goal_distribution = gaussian_local_balance * (
        1.0
        + (1.0 - diffusivity_ratio)
        * conductive_vector_slot
        * (relative_magnitude_square * inverse_level - 5.0)
        * inverse_scale
    )
    approach_rate = (
        encounter_rate * particle_concentration * kelvin_level ** (1.0 - power_law_index)
    )
    relaxed = advected_distribution + approach_rate * (
        corrected_goal_distribution - advected_distribution
    )
    magnitude_squares = (
        along_x_part * along_x_part + along_y_part * along_y_part + along_z_part * along_z_part
    )[:, None, None]
    wall_distribution = (
        particle_concentration
        * wall_kelvin ** (-1.5)
        * jnp.exp(-magnitude_squares / (2.0 * wall_kelvin))
    )
    inflow_magnitude_square = (
        (along_x_part - inflow_speed) ** 2
        + along_y_part * along_y_part
        + along_z_part * along_z_part
    )[:, None, None]
    inflow_distribution = (
        inflow_concentration
        * inflow_kelvin ** (-1.5)
        * jnp.exp(-inflow_magnitude_square / (2.0 * inflow_kelvin))
    )
    revised_distribution = jnp.where(
        kind_labels == 1,
        wall_distribution,
        jnp.where(kind_labels == 2, inflow_distribution, relaxed),
    )
    return (revised_distribution, kelvin_level)


def per_device(initial, site_kind):
    amount = initial.shape[0]
    along_x_part, along_y_part, along_z_part = speeds(lax.axis_index("vel") * amount, amount)
    distribution_table = initial
    kelvin_level = jnp.zeros(site_kind.shape, jnp.float32)
    signs = halo_signs(lax.axis_size("vel"), amount)
    for section in range(STEPS):
        if signs is None or distribution_table.shape[1] < 2:
            padded = with_halo(distribution_table, (("space", 1),), 2)
        else:
            padded = with_upwind_halo(distribution_table, signs)
        advected_distribution = transport(padded, along_x_part, along_y_part)
        distribution_table, kelvin_level = approach_increment(
            advected_distribution, site_kind, along_x_part, along_y_part, along_z_part
        )
    return (distribution_table, kelvin_level)


def solution(mesh):
    return jax.shard_map(
        per_device,
        mesh=mesh,
        in_specs=(P("vel", "space", None), P("space", None)),
        out_specs=(P("vel", "space", None), P("space", None)),
        check_vma=False,
    )
```

```python
import math

import jax
import numpy as np
import jax.numpy as jnp
from jax import lax
from jax.sharding import PartitionSpec as P

NVX = 24
STEPS = 2


speed_limit = 4.0
courant = 0.1
diffusivity_ratio = 2.0 / 3.0
power_law_index = 0.81
encounter_rate = 0.25
wall_kelvin = 1.0
inflow_concentration = 1.0
inflow_speed = 0.5
inflow_kelvin = 1.0


def with_halo(block, sides, width):
    for axis, dim in sides:
        count = lax.axis_size(axis)
        forward = [(i, i + 1) for i in range(count - 1)]
        backward = [(target, source) for source, target in forward]
        low = lax.ppermute(
            lax.slice_in_dim(block, block.shape[dim] - width, None, axis=dim), axis, forward
        )
        high = lax.ppermute(lax.slice_in_dim(block, 0, width, axis=dim), axis, backward)
        block = jnp.concatenate([low, block, high], axis=dim)
    return block


def halo_signs(vel_count, amount):
    spacing = 2.0 * speed_limit / (NVX - 1)
    signs = []
    for member in range(vel_count):
        index = np.arange(member * amount, (member + 1) * amount)
        along_x_part = np.float32(-speed_limit) + np.float32(spacing) * (index // (NVX * NVX)).astype(np.float32)
        if np.all(along_x_part > 0):
            signs.append(1)
        elif np.all(along_x_part < 0):
            signs.append(-1)
        else:
            return None
    return signs


def with_upwind_halo(block, signs):
    count = lax.axis_size("space")
    rows = block.shape[1]
    forward = [(i, i + 1) for i in range(count - 1)]
    backward = [(target, source) for source, target in forward]
    amount, _, width = block.shape
    flat = block.reshape(amount * rows, width)

    def row(index):
        return lax.slice(flat, (index, 0), (amount * rows, width), (rows, 1)).reshape(amount, 1, width)

    low = lax.ppermute(row(rows - 1), "space", forward)
    high = lax.ppermute(row(0), "space", backward)
    pairs = []
    for member, sign in enumerate(signs):
        for source, target in forward if sign > 0 else backward:
            pairs.append((member * count + source, member * count + target))
    positive = jnp.asarray(np.array(signs, np.int32))[lax.axis_index("vel")] > 0
    extra = lax.ppermute(
        jnp.where(positive, row(rows - 2), row(1)), ("vel", "space"), pairs
    )
    return jnp.concatenate([extra, low, block, high, extra], axis=1)


def speeds(offset, amount):
    index = offset + jnp.arange(amount, dtype=jnp.int32)
    spacing = 2.0 * speed_limit / (NVX - 1)
    along_x_part = -speed_limit + spacing * (index // (NVX * NVX)).astype(jnp.float32)
    along_y_part = -speed_limit + spacing * (index // NVX % NVX).astype(jnp.float32)
    along_z_part = -speed_limit + spacing * (index % NVX).astype(jnp.float32)
    return (along_x_part, along_y_part, along_z_part)


def quad_weight():
    return (2.0 * speed_limit / (NVX - 1)) ** 3 / (2.0 * math.pi) ** 1.5


def minmod(left, right):
    return jnp.maximum(jnp.minimum(left, right), jnp.minimum(jnp.maximum(left, right), 0.0))


def sweep(distribution_table, number, along):
    length = distribution_table.shape[along]

    def piece(source, low, high):
        return lax.slice_in_dim(source, low, high, axis=along)

    jumps = piece(distribution_table, 1, length) - piece(distribution_table, 0, length - 1)
    slopes = minmod(piece(jumps, 0, length - 2), piece(jumps, 1, length - 1))
    left_face = piece(distribution_table, 1, length - 2) + 0.5 * (1.0 - number) * piece(
        slopes, 0, length - 3
    )
    right_face = piece(distribution_table, 2, length - 1) - 0.5 * (1.0 + number) * piece(
        slopes, 1, length - 2
    )
    flux = number * jnp.where(number > 0, left_face, right_face)
    return piece(distribution_table, 2, length - 2) - (
        piece(flux, 1, length - 3) - piece(flux, 0, length - 4)
    )


def transport(padded, along_x_part, along_y_part):
    swept = sweep(padded, courant * along_x_part[:, None, None], 1)
    widened = jnp.pad(swept, ((0, 0), (0, 0), (2, 2)))
    return sweep(widened, courant * along_y_part[:, None, None], 2)


def xor_tree(values):
    while len(values) > 1:
        values = [values[2 * j] + values[2 * j + 1] for j in range(len(values) // 2)]
    return values[0]


def vel_sum(local):
    count = lax.axis_size("vel")
    if count & (count - 1):
        return lax.psum(local, "vel")
    bits = count.bit_length() - 1
    groups = []
    low = 0
    while low < bits:
        groups.append((low, min(2, bits - low)))
        low += 2
    for low, width in reversed(groups):
        values = [local]
        for member in range(1, 1 << width):
            mask = member << low
            values.append(lax.ppermute(local, "vel", [(i, i ^ mask) for i in range(count)]))
        local = xor_tree(values)
    return local


def macroscopic_moments(advected_distribution, along_x_part, along_y_part, along_z_part):
    magnitude_squares = (
        along_x_part * along_x_part + along_y_part * along_y_part + along_z_part * along_z_part
    )
    ones = jnp.ones_like(along_x_part)
    table = quad_weight() * jnp.stack(
        [
            ones,
            along_x_part,
            along_y_part,
            along_z_part,
            magnitude_squares,
            along_x_part * along_x_part,
            along_y_part * along_y_part,
            along_z_part * along_z_part,
            along_x_part * along_y_part,
            along_x_part * along_z_part,
            along_y_part * along_z_part,
            along_x_part * magnitude_squares,
            along_y_part * magnitude_squares,
            along_z_part * magnitude_squares,
            jnp.zeros_like(along_x_part),
            jnp.zeros_like(along_x_part),
        ]
    )
    local = jnp.einsum("kv,vrc->krc", table, advected_distribution, precision=lax.Precision.HIGHEST)
    totals = vel_sum(local)
    particle_concentration = totals[0]
    average_drift_x = totals[1] / particle_concentration
    average_drift_y = totals[2] / particle_concentration
    average_drift_z = totals[3] / particle_concentration
    energy = totals[4]
    drift_square = (
        average_drift_x * average_drift_x
        + average_drift_y * average_drift_y
        + average_drift_z * average_drift_z
    )
    kelvin_level = (energy / particle_concentration - drift_square) / 3.0
    xx, yy, zz, xy, xz, yz = (totals[k] for k in range(5, 11))
    drift = (average_drift_x, average_drift_y, average_drift_z)
    second = ((xx, xy, xz), (xy, yy, yz), (xz, yz, zz))
    common = 2.0 * particle_concentration * drift_square
    conductive_transfer = jnp.stack(
        [
            0.5
            * (
                totals[11 + i]
                - 2.0 * (drift[0] * second[i][0] + drift[1] * second[i][1] + drift[2] * second[i][2])
                - drift[i] * energy
                + drift[i] * common
            )
            for i in range(3)
        ]
    )
    return (
        particle_concentration,
        average_drift_x,
        average_drift_y,
        average_drift_z,
        kelvin_level,
        conductive_transfer,
    )


def approach_increment(
    advected_distribution, kind_labels, along_x_part, along_y_part, along_z_part
):
    (
        particle_concentration,
        average_drift_x,
        average_drift_y,
        average_drift_z,
        kelvin_level,
        conductive_transfer,
    ) = macroscopic_moments(advected_distribution, along_x_part, along_y_part, along_z_part)
    rel_x = along_x_part[:, None, None] - average_drift_x[None]
    rel_y = along_y_part[:, None, None] - average_drift_y[None]
    rel_z = along_z_part[:, None, None] - average_drift_z[None]
    relative_magnitude_square = rel_x * rel_x + rel_y * rel_y + rel_z * rel_z
    stress_scalar_grid = particle_concentration * kelvin_level
    gaussian_local_balance = (
        particle_concentration
        * kelvin_level ** (-1.5)
        * jnp.exp(-relative_magnitude_square / (2.0 * kelvin_level))
    )
    conductive_vector_slot = (
        rel_x * conductive_transfer[0]
        + rel_y * conductive_transfer[1]
        + rel_z * conductive_transfer[2]
    )
    corrected_goal_distribution = gaussian_local_balance * (
        1.0
        + (1.0 - diffusivity_ratio)
        * conductive_vector_slot
        * (relative_magnitude_square / kelvin_level - 5.0)
        / (5.0 * stress_scalar_grid * kelvin_level)
    )
    approach_rate = (
        encounter_rate * particle_concentration * kelvin_level ** (1.0 - power_law_index)
    )
    relaxed = advected_distribution + approach_rate * (
        corrected_goal_distribution - advected_distribution
    )
    magnitude_squares = (
        along_x_part * along_x_part + along_y_part * along_y_part + along_z_part * along_z_part
    )[:, None, None]
    wall_distribution = (
        particle_concentration
        * wall_kelvin ** (-1.5)
        * jnp.exp(-magnitude_squares / (2.0 * wall_kelvin))
    )
    inflow_magnitude_square = (
        (along_x_part - inflow_speed) ** 2
        + along_y_part * along_y_part
        + along_z_part * along_z_part
    )[:, None, None]
    inflow_distribution = (
        inflow_concentration
        * inflow_kelvin ** (-1.5)
        * jnp.exp(-inflow_magnitude_square / (2.0 * inflow_kelvin))
    )
    revised_distribution = jnp.where(
        kind_labels == 1,
        wall_distribution,
        jnp.where(kind_labels == 2, inflow_distribution, relaxed),
    )
    return (revised_distribution, kelvin_level)


def per_device(initial, site_kind):
    amount = initial.shape[0]
    along_x_part, along_y_part, along_z_part = speeds(lax.axis_index("vel") * amount, amount)
    distribution_table = initial
    kelvin_level = jnp.zeros(site_kind.shape, jnp.float32)
    signs = halo_signs(lax.axis_size("vel"), amount)
    for section in range(STEPS):
        if signs is None or distribution_table.shape[1] < 2:
            padded = with_halo(distribution_table, (("space", 1),), 2)
        else:
            padded = with_upwind_halo(distribution_table, signs)
        advected_distribution = transport(padded, along_x_part, along_y_part)
        distribution_table, kelvin_level = approach_increment(
            advected_distribution, site_kind, along_x_part, along_y_part, along_z_part
        )
    return (distribution_table, kelvin_level)


def solution(mesh):
    return jax.shard_map(
        per_device,
        mesh=mesh,
        in_specs=(P("vel", "space", None), P("space", None)),
        out_specs=(P("vel", "space", None), P("space", None)),
        check_vma=False,
    )
```

```python
import math

import jax
import numpy as np
import jax.numpy as jnp
from jax import lax
from jax.sharding import PartitionSpec as P

NVX = 24
STEPS = 2


speed_limit = 4.0
courant = 0.1
diffusivity_ratio = 2.0 / 3.0
power_law_index = 0.81
encounter_rate = 0.25
wall_kelvin = 1.0
inflow_concentration = 1.0
inflow_speed = 0.5
inflow_kelvin = 1.0


def with_halo(block, sides, width):
    for axis, dim in sides:
        count = lax.axis_size(axis)
        forward = [(i, i + 1) for i in range(count - 1)]
        backward = [(target, source) for source, target in forward]
        low = lax.ppermute(
            lax.slice_in_dim(block, block.shape[dim] - width, None, axis=dim), axis, forward
        )
        high = lax.ppermute(lax.slice_in_dim(block, 0, width, axis=dim), axis, backward)
        block = jnp.concatenate([low, block, high], axis=dim)
    return block


def halo_signs(vel_count, amount):
    spacing = 2.0 * speed_limit / (NVX - 1)
    signs = []
    for member in range(vel_count):
        index = np.arange(member * amount, (member + 1) * amount)
        along_x_part = np.float32(-speed_limit) + np.float32(spacing) * (index // (NVX * NVX)).astype(np.float32)
        if np.all(along_x_part > 0):
            signs.append(1)
        elif np.all(along_x_part < 0):
            signs.append(-1)
        else:
            return None
    return signs


def with_upwind_halo(block, signs):
    count = lax.axis_size("space")
    rows = block.shape[1]
    forward = [(i, i + 1) for i in range(count - 1)]
    backward = [(target, source) for source, target in forward]
    low = lax.ppermute(block[:, rows - 1 :], "space", forward)
    high = lax.ppermute(block[:, :1], "space", backward)
    pairs = []
    for member, sign in enumerate(signs):
        for source, target in forward if sign > 0 else backward:
            pairs.append((member * count + source, member * count + target))
    positive = jnp.asarray(np.array(signs, np.int32))[lax.axis_index("vel")] > 0
    extra = lax.ppermute(
        jnp.where(positive, block[:, rows - 2 : rows - 1], block[:, 1:2]), ("vel", "space"), pairs
    )
    return jnp.concatenate([extra, low, block, high, extra], axis=1)


def speeds(offset, amount):
    index = offset + jnp.arange(amount, dtype=jnp.int32)
    spacing = 2.0 * speed_limit / (NVX - 1)
    along_x_part = -speed_limit + spacing * (index // (NVX * NVX)).astype(jnp.float32)
    along_y_part = -speed_limit + spacing * (index // NVX % NVX).astype(jnp.float32)
    along_z_part = -speed_limit + spacing * (index % NVX).astype(jnp.float32)
    return (along_x_part, along_y_part, along_z_part)


def quad_weight():
    return (2.0 * speed_limit / (NVX - 1)) ** 3 / (2.0 * math.pi) ** 1.5


def minmod(left, right):
    return jnp.maximum(jnp.minimum(left, right), jnp.minimum(jnp.maximum(left, right), 0.0))


def sweep(distribution_table, number, along):
    length = distribution_table.shape[along]

    def piece(source, low, high):
        return lax.slice_in_dim(source, low, high, axis=along)

    jumps = piece(distribution_table, 1, length) - piece(distribution_table, 0, length - 1)
    slopes = minmod(piece(jumps, 0, length - 2), piece(jumps, 1, length - 1))
    left_face = piece(distribution_table, 1, length - 2) + 0.5 * (1.0 - number) * piece(
        slopes, 0, length - 3
    )
    right_face = piece(distribution_table, 2, length - 1) - 0.5 * (1.0 + number) * piece(
        slopes, 1, length - 2
    )
    flux = number * jnp.where(number > 0, left_face, right_face)
    return piece(distribution_table, 2, length - 2) - (
        piece(flux, 1, length - 3) - piece(flux, 0, length - 4)
    )


def transport(padded, along_x_part, along_y_part):
    swept = sweep(padded, courant * along_x_part[:, None, None], 1)
    widened = jnp.pad(swept, ((0, 0), (0, 0), (2, 2)))
    return sweep(widened, courant * along_y_part[:, None, None], 2)


def xor_tree(values):
    while len(values) > 1:
        values = [values[2 * j] + values[2 * j + 1] for j in range(len(values) // 2)]
    return values[0]


def vel_sum(local):
    count = lax.axis_size("vel")
    if count & (count - 1):
        return lax.psum(local, "vel")
    bits = count.bit_length() - 1
    groups = []
    low = 0
    while low < bits:
        groups.append((low, min(2, bits - low)))
        low += 2
    for low, width in reversed(groups):
        values = [local]
        for member in range(1, 1 << width):
            mask = member << low
            values.append(lax.ppermute(local, "vel", [(i, i ^ mask) for i in range(count)]))
        local = xor_tree(values)
    return local


def macroscopic_moments(advected_distribution, along_x_part, along_y_part, along_z_part):
    magnitude_squares = (
        along_x_part * along_x_part + along_y_part * along_y_part + along_z_part * along_z_part
    )
    ones = jnp.ones_like(along_x_part)
    table = quad_weight() * jnp.stack(
        [
            ones,
            along_x_part,
            along_y_part,
            along_z_part,
            magnitude_squares,
            along_x_part * along_x_part,
            along_y_part * along_y_part,
            along_z_part * along_z_part,
            along_x_part * along_y_part,
            along_x_part * along_z_part,
            along_y_part * along_z_part,
            along_x_part * magnitude_squares,
            along_y_part * magnitude_squares,
            along_z_part * magnitude_squares,
            jnp.zeros_like(along_x_part),
            jnp.zeros_like(along_x_part),
        ]
    )
    local = jnp.einsum("kv,vrc->krc", table, advected_distribution, precision=lax.Precision.HIGH)
    totals = vel_sum(local)
    particle_concentration = totals[0]
    average_drift_x = totals[1] / particle_concentration
    average_drift_y = totals[2] / particle_concentration
    average_drift_z = totals[3] / particle_concentration
    energy = totals[4]
    drift_square = (
        average_drift_x * average_drift_x
        + average_drift_y * average_drift_y
        + average_drift_z * average_drift_z
    )
    kelvin_level = (energy / particle_concentration - drift_square) / 3.0
    xx, yy, zz, xy, xz, yz = (totals[k] for k in range(5, 11))
    drift = (average_drift_x, average_drift_y, average_drift_z)
    second = ((xx, xy, xz), (xy, yy, yz), (xz, yz, zz))
    common = 2.0 * particle_concentration * drift_square
    conductive_transfer = jnp.stack(
        [
            0.5
            * (
                totals[11 + i]
                - 2.0 * (drift[0] * second[i][0] + drift[1] * second[i][1] + drift[2] * second[i][2])
                - drift[i] * energy
                + drift[i] * common
            )
            for i in range(3)
        ]
    )
    return (
        particle_concentration,
        average_drift_x,
        average_drift_y,
        average_drift_z,
        kelvin_level,
        conductive_transfer,
    )


def approach_increment(
    advected_distribution, kind_labels, along_x_part, along_y_part, along_z_part
):
    (
        particle_concentration,
        average_drift_x,
        average_drift_y,
        average_drift_z,
        kelvin_level,
        conductive_transfer,
    ) = macroscopic_moments(advected_distribution, along_x_part, along_y_part, along_z_part)
    rel_x = along_x_part[:, None, None] - average_drift_x[None]
    rel_y = along_y_part[:, None, None] - average_drift_y[None]
    rel_z = along_z_part[:, None, None] - average_drift_z[None]
    relative_magnitude_square = rel_x * rel_x + rel_y * rel_y + rel_z * rel_z
    stress_scalar_grid = particle_concentration * kelvin_level
    gaussian_local_balance = (
        particle_concentration
        * kelvin_level ** (-1.5)
        * jnp.exp(-relative_magnitude_square / (2.0 * kelvin_level))
    )
    conductive_vector_slot = (
        rel_x * conductive_transfer[0]
        + rel_y * conductive_transfer[1]
        + rel_z * conductive_transfer[2]
    )
    corrected_goal_distribution = gaussian_local_balance * (
        1.0
        + (1.0 - diffusivity_ratio)
        * conductive_vector_slot
        * (relative_magnitude_square / kelvin_level - 5.0)
        / (5.0 * stress_scalar_grid * kelvin_level)
    )
    approach_rate = (
        encounter_rate * particle_concentration * kelvin_level ** (1.0 - power_law_index)
    )
    relaxed = advected_distribution + approach_rate * (
        corrected_goal_distribution - advected_distribution
    )
    magnitude_squares = (
        along_x_part * along_x_part + along_y_part * along_y_part + along_z_part * along_z_part
    )[:, None, None]
    wall_distribution = (
        particle_concentration
        * wall_kelvin ** (-1.5)
        * jnp.exp(-magnitude_squares / (2.0 * wall_kelvin))
    )
    inflow_magnitude_square = (
        (along_x_part - inflow_speed) ** 2
        + along_y_part * along_y_part
        + along_z_part * along_z_part
    )[:, None, None]
    inflow_distribution = (
        inflow_concentration
        * inflow_kelvin ** (-1.5)
        * jnp.exp(-inflow_magnitude_square / (2.0 * inflow_kelvin))
    )
    revised_distribution = jnp.where(
        kind_labels == 1,
        wall_distribution,
        jnp.where(kind_labels == 2, inflow_distribution, relaxed),
    )
    return (revised_distribution, kelvin_level)


def per_device(initial, site_kind):
    amount = initial.shape[0]
    along_x_part, along_y_part, along_z_part = speeds(lax.axis_index("vel") * amount, amount)
    distribution_table = initial
    kelvin_level = jnp.zeros(site_kind.shape, jnp.float32)
    signs = halo_signs(lax.axis_size("vel"), amount)
    for section in range(STEPS):
        if signs is None or distribution_table.shape[1] < 2:
            padded = with_halo(distribution_table, (("space", 1),), 2)
        else:
            padded = with_upwind_halo(distribution_table, signs)
        advected_distribution = transport(padded, along_x_part, along_y_part)
        distribution_table, kelvin_level = approach_increment(
            advected_distribution, site_kind, along_x_part, along_y_part, along_z_part
        )
    return (distribution_table, kelvin_level)


def solution(mesh):
    return jax.shard_map(
        per_device,
        mesh=mesh,
        in_specs=(P("vel", "space", None), P("space", None)),
        out_specs=(P("vel", "space", None), P("space", None)),
        check_vma=False,
    )
```
